256 devices in a mesh: sec: 8 (over z), blk: 32 (over y, x, core).
Axes of the slice: x: 4, y: 4, z: 8, core: 2. Of those that a mesh axis runs over, the one named last changes fastest.
Arguments:
- guess: bfloat16 [8, 32, 128, 32, 128], P('sec', None, None, 'blk'), may hold values from -6 to 6
- left_env: bfloat16 [8, 2, 32, 128, 128], P('sec', None, 'blk'), as said below
- right_env: bfloat16 [8, 2, 32, 128, 128], P('sec', None, 'blk'), as said below
- left_dims: int32 [8, 32], P('sec'), may hold values from 1 to 128, as said below
- right_dims: int32 [8, 32], P('sec'), may hold values from 1 to 128, as said below
- left_labels: int32 [8, 32], P('sec'), may hold values from 0 to 4, as said below
- right_labels: int32 [8, 32], P('sec'), may hold values from 0 to 4, as said below
Outputs:
- waves: float32 [8, 32, 128, 32, 128], P('sec', None, None, 'blk')
- energies: float32 [8, 2], P('sec')
The draws below stay inside these ranges and needn't reach their ends.
Inputs may be any that keep to these rules, and one draw needn't show every extreme that they name: `left_env`: every block of the environments is symmetric in its last two dimensions. `right_env`: every block of the environments is symmetric in its last two dimensions. `left_dims`: some sector of every section has all 128 states live. The left sectors of section s are the right sectors of section s - 1, with the same sizes. `right_dims`: some sector of every section has all 128 states live. `left_labels`: the left labels of section s are the right labels of section s - 1. Every particle number from 0 to 4 labels some sector of every bond. `right_labels`: every particle number from 0 to 4 labels some sector of every bond.
All inputs are finite; a program needn't handle non-finite values.
Results may differ from the reference program's by a relative error of at most 0.012.
Values may be sent and summed in bfloat16 or wider, within the bound.
No kernel may reach another device: no remote copies, remote signals or barrier semaphores. Data moves between devices by JAX's collectives and lax.ppermute only.
A program may use at most 64 MiB of HBM per device.

```python
import jax
import jax.numpy as jnp
from jax import lax

BS = 128
W = 2
ITERS = 2
NSEC = 32
STATES = 4096
SECTIONS = 8


def symmetric_blocks(key):
    shape = (SECTIONS, W, NSEC, BS, BS)
    noise = jax.random.normal(key, shape, jnp.float32)
    return ((noise + jnp.swapaxes(noise, 3, 4)) * (0.5 / BS) ** 0.5).astype(jnp.bfloat16)


def boundary_ints(key):
    sizes_key = jax.random.fold_in(key, 101)
    position_key = jax.random.fold_in(key, 102)
    label_key = jax.random.fold_in(key, 103)
    sector_sizes = jax.random.randint(sizes_key, (SECTIONS + 1, NSEC), BS // 2, BS + 1)
    position = jax.random.randint(position_key, (SECTIONS + 1, 1), 0, NSEC)
    indices = jnp.arange(NSEC, dtype=jnp.int32)[None, :]
    sector_sizes = jnp.where(indices == position, BS, sector_sizes).astype(jnp.int32)
    label_keys = jax.random.split(label_key, SECTIONS + 1)
    orders = jax.vmap(lambda one_key: jax.random.permutation(one_key, NSEC))(label_keys)
    labels = (orders % 5).astype(jnp.int32)
    return (sector_sizes, labels)


def draw_left_env(key, part):
    return symmetric_blocks(jax.random.fold_in(key, 5))


def draw_right_env(key, part):
    return symmetric_blocks(jax.random.fold_in(key, 6))


def draw_left_dims(key, part):
    return boundary_ints(key)[0][:SECTIONS]


def draw_right_dims(key, part):
    return boundary_ints(key)[0][1:]


def draw_left_labels(key, part):
    return boundary_ints(key)[1][:SECTIONS]


def draw_right_labels(key, part):
    return boundary_ints(key)[1][1:]


def shard_levels(key, extent, cuts, low, largest):
    factor_of = 1.0
    for axis_at, parts in cuts:
        draws = jax.random.uniform(jax.random.fold_in(jax.random.fold_in(key, 6), axis_at), (parts,), jnp.float32, low / len(cuts), largest / len(cuts))
        factor_of = factor_of * jnp.repeat(jnp.exp(draws), extent[axis_at] // parts).reshape((-1,) + (1,) * (len(extent) - 1 - axis_at))
    return factor_of


def centred(stream_key, dims, deviation, reach, cuts=(), kind=jnp.bfloat16):
    array = deviation * jax.random.normal(stream_key, dims, jnp.float32)
    if cuts:
        array = array * shard_levels(stream_key, dims, cuts, -0.22, 0.18)
    return jnp.clip(array, -reach, reach).astype(kind)


def setup_inputs(seed: int = 0) -> dict:
    streams_of = jax.random.split(jax.random.key(seed), 8)
    guess = centred(streams_of[0], (SECTIONS, NSEC, BS, NSEC, BS), 1.0, 6.0, ((0, 8), (3, 32)))
    left_env = draw_left_env(jax.random.fold_in(streams_of[7], 71), 0)
    right_env = draw_right_env(jax.random.fold_in(streams_of[7], 71), 0)
    left_dims = draw_left_dims(jax.random.fold_in(streams_of[7], 71), 0)
    right_dims = draw_right_dims(jax.random.fold_in(streams_of[7], 71), 0)
    left_labels = draw_left_labels(jax.random.fold_in(streams_of[7], 71), 0)
    right_labels = draw_right_labels(jax.random.fold_in(streams_of[7], 71), 0)
    return {"guess": guess, "left_env": left_env, "right_env": right_env, "left_dims": left_dims, "right_dims": right_dims, "left_labels": left_labels, "right_labels": right_labels}


EPS = 1e-06

def block_mask(left_sizes, right_sizes, left_marks, right_marks, block_size):
    total = left_marks[:, None] + right_marks[None, :]
    allowed = (total == 4).astype(jnp.float32)
    offsets = jnp.arange(block_size, dtype=jnp.int32)
    live_rows = (offsets[None, :] < left_sizes[:, None]).astype(jnp.float32)
    live_cols = (offsets[None, :] < right_sizes[:, None]).astype(jnp.float32)
    return allowed[:, None, :, None] * live_rows[:, :, None, None] * live_cols[None, None, :, :]

def rounded_copy(vector):
    return lax.optimization_barrier(vector.astype(jnp.bfloat16)).astype(jnp.float32)

def left_product(rounded, left_block):
    return jnp.einsum('wqac,qcrb->wqarb', left_block.astype(jnp.float32), rounded).astype(jnp.bfloat16)

def hamiltonian(vector, left_block, right_block, pattern):
    left_done = left_product(rounded_copy(vector), left_block)
    return jnp.einsum('wqarc,wrbc->qarb', left_done.astype(jnp.float32), right_block.astype(jnp.float32)) * pattern

def davidson(start, left_block, right_block, pattern):
    vector = start.astype(jnp.float32) * pattern
    vector = vector / jnp.sqrt(jnp.sum(vector * vector) + EPS)
    image = hamiltonian(vector, left_block, right_block, pattern)
    ritz_value = jnp.sum(vector * image)
    for sweep in range(ITERS):
        residual = image - ritz_value * vector
        response = hamiltonian(residual, left_block, right_block, pattern)
        squared = jnp.sum(residual * residual) + EPS
        coupling = jnp.sum(residual * response) / squared
        midpoint = 0.5 * (ritz_value - coupling)
        radius = jnp.sqrt(midpoint * midpoint + squared)
        cosine = jnp.sqrt(0.5 * (1.0 - midpoint / radius))
        sine_value = -jnp.sqrt(0.5 * (1.0 + midpoint / radius))
        length = jnp.sqrt(squared)
        vector = cosine * vector + sine_value / length * residual
        image = cosine * image + sine_value / length * response
        ritz_value = 0.5 * (ritz_value + coupling) - radius
    return (vector, ritz_value)

def refresh(vector, left_block):
    rounded = rounded_copy(vector)
    left_done = left_product(rounded, left_block)
    return (STATES * jnp.einsum('qarb,wqarc->wrbc', rounded, left_done.astype(jnp.float32))).astype(jnp.bfloat16)

def reference(guess, left_env, right_env, left_dims, right_dims, left_labels, right_labels):
    first_vectors = []
    first_values = []
    freshes = []
    for section in range(SECTIONS):
        pattern = block_mask(left_dims[section], right_dims[section], left_labels[section], right_labels[section], BS)
        vector, value = davidson(guess[section], left_env[section], right_env[section], pattern)
        first_vectors.append(vector)
        first_values.append(value)
        freshes.append(refresh(vector, left_env[section]))
    waves = []
    energies = []
    for section in range(SECTIONS):
        pattern = block_mask(left_dims[section], right_dims[section], left_labels[section], right_labels[section], BS)
        if section == 0:
            second_left = left_env[0]
        else:
            second_left = freshes[section - 1]
        vector, value = davidson(first_vectors[section], second_left, right_env[section], pattern)
        waves.append(STATES * vector)
        energies.append(jnp.stack([first_values[section], value]))
    return (jnp.stack(waves), jnp.stack(energies))
```

```python
import jax
import jax.numpy as jnp
from jax import lax
from jax.sharding import PartitionSpec as P

ITERS = 2


EPS = 1e-06


def group_sum(value, axis):
    size = lax.axis_size(axis)
    stages = []
    stride = 1
    for radix in (2, 4, 4, 2, 2, 2, 2):
        if stride >= size:
            break
        if size % (stride * radix):
            radix = 2
        stages.append((radix, stride))
        stride *= radix
    position = lax.axis_index(axis)
    total = value
    for radix, stride in stages:
        digit = (position // stride) % radix
        received = [total]
        for shift in range(1, radix):
            route = []
            for source in range(size):
                own = (source // stride) % radix
                route.append((source, source + (((own + shift) % radix) - own) * stride))
            received.append(lax.ppermute(total, axis, route))
        stacked = jnp.stack(received)
        ordered = [stacked[(digit - origin) % radix] for origin in range(radix)]
        total = ordered[0]
        for part in ordered[1:]:
            total = total + part
    return total


def from_behind(block, axis, distance):
    devices = range(lax.axis_size(axis))
    route = [(i - distance, i) for i in devices if i - distance in devices]
    return lax.ppermute(block, axis, route)


def block_mask(left_sizes, right_sizes, left_marks, right_marks, block_size):
    total = left_marks[:, None] + right_marks[None, :]
    allowed = (total == 4).astype(jnp.float32)
    offsets = jnp.arange(block_size, dtype=jnp.int32)
    live_rows = (offsets[None, :] < left_sizes[:, None]).astype(jnp.float32)
    live_cols = (offsets[None, :] < right_sizes[:, None]).astype(jnp.float32)
    return allowed[:, None, :, None] * live_rows[:, :, None, None] * live_cols[None, None, :, :]


def left_product(left_block):
    gathered = lax.all_gather(left_block, "blk", axis=1, tiled=True)

    def product(rounded):
        return jnp.einsum(
            "wqac,qcrb->wqarb", gathered, rounded, preferred_element_type=jnp.float32
        ).astype(jnp.bfloat16)

    return product


def hamiltonian(product, right_block, pattern):

    def apply_all(vector):
        left_done = product(vector.astype(jnp.bfloat16))
        return (
            jnp.einsum(
                "wqarc,wrbc->qarb", left_done, right_block, preferred_element_type=jnp.float32
            )
            * pattern
        )

    return apply_all


def davidson(start, apply_all, pattern):
    vector = start * pattern
    total = group_sum(jnp.sum(vector * vector), "blk")
    vector = vector / jnp.sqrt(total + EPS)
    image = apply_all(vector)
    ritz_value = group_sum(jnp.sum(vector * image), "blk")
    for sweep in range(ITERS):
        residual = image - ritz_value * vector
        response = apply_all(residual)
        sums = group_sum(
            jnp.stack([jnp.sum(residual * residual), jnp.sum(residual * response)]), "blk"
        )
        squared = sums[0] + EPS
        correlation = sums[1]
        coupling = correlation / squared
        midpoint = 0.5 * (ritz_value - coupling)
        radius = jnp.sqrt(midpoint * midpoint + squared)
        cosine = jnp.sqrt(0.5 * (1.0 - midpoint / radius))
        sine_value = -jnp.sqrt(0.5 * (1.0 + midpoint / radius))
        length = jnp.sqrt(squared)
        vector = cosine * vector + sine_value / length * residual
        image = cosine * image + sine_value / length * response
        ritz_value = 0.5 * (ritz_value + coupling) - radius
    return (vector, ritz_value)


def refresh(vector, product, states):
    rounded = vector.astype(jnp.bfloat16)
    left_done = product(rounded)
    return (
        states
        * jnp.einsum("qarb,wqarc->wrbc", rounded, left_done, preferred_element_type=jnp.float32)
    ).astype(jnp.bfloat16)


def local(guess, left_env, right_env, left_dims, right_dims, left_labels, right_labels):
    start_guess = guess[0].astype(jnp.float32)
    left_block = left_env[0]
    right_block = right_env[0]
    sector_count = start_guess.shape[0]
    block_size = start_guess.shape[1]
    owned_count = start_guess.shape[2]
    states = sector_count * block_size
    first_owned = lax.axis_index("blk") * owned_count
    owned_sizes = lax.dynamic_slice_in_dim(right_dims[0], first_owned, owned_count, 0)
    owned_marks = lax.dynamic_slice_in_dim(right_labels[0], first_owned, owned_count, 0)
    pattern = block_mask(left_dims[0], owned_sizes, left_labels[0], owned_marks, block_size)
    first_product = left_product(left_block)
    first_vector, first_energy = davidson(
        start_guess, hamiltonian(first_product, right_block, pattern), pattern
    )
    fresh = refresh(first_vector, first_product, states)
    passed = from_behind(fresh, "sec", 1)
    second_left = jnp.where(lax.axis_index("sec") == 0, left_block, passed)
    second_product = left_product(second_left)
    second_vector, second_energy = davidson(
        first_vector, hamiltonian(second_product, right_block, pattern), pattern
    )
    waves = (states * second_vector)[None]
    energies = jnp.stack([first_energy, second_energy])[None]
    return (waves, energies)


def solution(mesh):
    return jax.shard_map(
        local,
        mesh=mesh,
        in_specs=(
            P("sec", None, None, "blk", None),
            P("sec", None, "blk", None, None),
            P("sec", None, "blk", None, None),
            P("sec", None),
            P("sec", None),
            P("sec", None),
            P("sec", None),
        ),
        out_specs=(P("sec", None, None, "blk", None), P("sec", None)),
        check_vma=False,
    )
```

```python
import jax
import jax.numpy as jnp
from jax import lax
from jax.sharding import PartitionSpec as P

ITERS = 2


EPS = 1e-06


def group_reduce(value, axis, combine):
    size = lax.axis_size(axis)
    stages = []
    stride = 1
    for radix in (2, 4, 4, 2, 2, 2, 2):
        if stride >= size:
            break
        if size % (stride * radix):
            radix = 2
        stages.append((radix, stride))
        stride *= radix
    position = lax.axis_index(axis)
    total = value
    for radix, stride in stages:
        digit = (position // stride) % radix
        received = [total]
        for shift in range(1, radix):
            route = []
            for source in range(size):
                own = (source // stride) % radix
                route.append((source, source + (((own + shift) % radix) - own) * stride))
            received.append(lax.ppermute(total, axis, route))
        stacked = jnp.stack(received)
        ordered = [stacked[(digit - origin) % radix] for origin in range(radix)]
        total = ordered[0]
        for part in ordered[1:]:
            total = combine(total, part)
    return total


def from_behind(block, axis, distance):
    devices = range(lax.axis_size(axis))
    route = [(i - distance, i) for i in devices if i - distance in devices]
    return lax.ppermute(block, axis, route)


def block_mask(left_sizes, right_sizes, left_marks, right_marks, block_size):
    total = left_marks[:, None] + right_marks[None, :]
    allowed = (total == 4).astype(jnp.float32)
    offsets = jnp.arange(block_size, dtype=jnp.int32)
    live_rows = (offsets[None, :] < left_sizes[:, None]).astype(jnp.float32)
    live_cols = (offsets[None, :] < right_sizes[:, None]).astype(jnp.float32)
    return allowed[:, None, :, None] * live_rows[:, :, None, None] * live_cols[None, None, :, :]


def left_product(gathered):

    def product(rounded):
        return jnp.einsum(
            "wqac,qcrb->wqarb", gathered, rounded, preferred_element_type=jnp.float32
        ).astype(jnp.bfloat16)

    return product


def hamiltonian(product, right_block, pattern):

    def apply_all(vector):
        left_done = product(vector.astype(jnp.bfloat16))
        return (
            jnp.einsum(
                "wqarc,wrbc->qarb", left_done, right_block, preferred_element_type=jnp.float32
            )
            * pattern
        )

    return apply_all


def operator_bound(left_peak, right_peak, block_size):
    bound = jnp.sum((block_size * left_peak) * (block_size * right_peak))
    bound = jnp.minimum(bound, jnp.finfo(jnp.float32).max)
    return jnp.where(bound > 0, bound, 1.0)


def krylov(first, apply_all, bound):
    basis = [first, apply_all(first)]
    for step in range(ITERS):
        basis.append(apply_all(basis[-1]) / bound)
    count = len(basis)
    pairs = [(i, j) for i in range(count) for j in range(i, count)]
    partial = jnp.stack([jnp.sum(basis[i] * basis[j]) for i, j in pairs])
    gram_sums = group_reduce(partial, "blk", lambda a, b: a + b)
    rows = [[None] * count for _ in range(count)]
    for index, (i, j) in enumerate(pairs):
        rows[i][j] = gram_sums[index]
        rows[j][i] = gram_sums[index]
    gram = jnp.stack([jnp.stack(row) for row in rows])
    return basis, gram


def rotations(gram, bound):
    count = gram.shape[0]

    def inner(x, y):
        return jnp.sum(x[:, None] * gram * y[None, :])

    def shift(x):
        scaled = x[:-1] * jnp.concatenate([jnp.ones((1,), jnp.float32), jnp.full((count - 2,), bound)])
        return jnp.concatenate([jnp.zeros((1,), jnp.float32), scaled])

    unit = jnp.eye(count, dtype=jnp.float32)
    vector = unit[0]
    image = unit[1]
    ritz_value = inner(vector, image)
    for sweep in range(ITERS):
        residual = image - ritz_value * vector
        response = shift(residual)
        squared = inner(residual, residual) + EPS
        coupling = inner(residual, response) / squared
        midpoint = 0.5 * (ritz_value - coupling)
        radius = jnp.sqrt(midpoint * midpoint + squared)
        cosine = jnp.sqrt(0.5 * (1.0 - midpoint / radius))
        sine_value = -jnp.sqrt(0.5 * (1.0 + midpoint / radius))
        length = jnp.sqrt(squared)
        vector = cosine * vector + sine_value / length * residual
        image = cosine * image + sine_value / length * response
        ritz_value = 0.5 * (ritz_value + coupling) - radius
    return vector, ritz_value


def davidson(first, apply_all, bound):
    basis, gram = krylov(first, apply_all, bound)
    weights, ritz_value = rotations(gram, bound)
    vector = weights[0] * basis[0]
    for k in range(1, len(basis) - 1):
        vector = vector + weights[k] * basis[k]
    norm_sq = jnp.sum(weights[:, None] * gram * weights[None, :])
    return vector, ritz_value, norm_sq


def refresh(vector, product, states):
    rounded = vector.astype(jnp.bfloat16)
    left_done = product(rounded)
    return (
        states
        * jnp.einsum("qarb,wqarc->wrbc", rounded, left_done, preferred_element_type=jnp.float32)
    ).astype(jnp.bfloat16)


def peak(block):
    return jnp.max(jnp.abs(block.astype(jnp.float32)), axis=(1, 2, 3))


def local(guess, left_env, right_env, left_dims, right_dims, left_labels, right_labels):
    start_guess = guess[0].astype(jnp.float32)
    left_block = left_env[0]
    right_block = right_env[0]
    sector_count = start_guess.shape[0]
    block_size = start_guess.shape[1]
    owned_count = start_guess.shape[2]
    states = sector_count * block_size
    first_owned = lax.axis_index("blk") * owned_count
    owned_sizes = lax.dynamic_slice_in_dim(right_dims[0], first_owned, owned_count, 0)
    owned_marks = lax.dynamic_slice_in_dim(right_labels[0], first_owned, owned_count, 0)
    pattern = block_mask(left_dims[0], owned_sizes, left_labels[0], owned_marks, block_size)
    masked = start_guess * pattern
    early = group_reduce(
        jnp.concatenate([jnp.sum(masked * masked)[None], peak(right_block)]),
        "blk",
        lambda a, b: jnp.concatenate([a[:1] + b[:1], jnp.maximum(a[1:], b[1:])]),
    )
    right_peak = early[1:]
    first_gathered = lax.all_gather(left_block, "blk", axis=1, tiled=True)
    first_product = left_product(first_gathered)
    first_bound = operator_bound(peak(first_gathered), right_peak, block_size)
    first_start = masked / jnp.sqrt(early[0] + EPS)
    first_vector, first_energy, first_norm = davidson(
        first_start, hamiltonian(first_product, right_block, pattern), first_bound
    )
    fresh = refresh(first_vector, first_product, states)
    passed = from_behind(fresh, "sec", 1)
    second_left = jnp.where(lax.axis_index("sec") == 0, left_block, passed)
    second_gathered = lax.all_gather(second_left, "blk", axis=1, tiled=True)
    second_product = left_product(second_gathered)
    second_bound = operator_bound(peak(second_gathered), right_peak, block_size)
    second_start = first_vector * pattern / jnp.sqrt(first_norm + EPS)
    second_vector, second_energy, _ = davidson(
        second_start, hamiltonian(second_product, right_block, pattern), second_bound
    )
    waves = (states * second_vector)[None]
    energies = jnp.stack([first_energy, second_energy])[None]
    return (waves, energies)


def solution(mesh):
    return jax.shard_map(
        local,
        mesh=mesh,
        in_specs=(
            P("sec", None, None, "blk", None),
            P("sec", None, "blk", None, None),
            P("sec", None, "blk", None, None),
            P("sec", None),
            P("sec", None),
            P("sec", None),
            P("sec", None),
        ),
        out_specs=(P("sec", None, None, "blk", None), P("sec", None)),
        check_vma=False,
    )
```

```python
import jax
import jax.numpy as jnp
from jax import lax
from jax.sharding import PartitionSpec as P

ITERS = 2


EPS = 1e-06


def radix_stages(size):
    stages = []
    stride = 1
    for radix in (2, 4, 4, 2, 2, 2, 2):
        if stride >= size:
            break
        if size % (stride * radix):
            radix = 2
        stages.append((radix, stride))
        stride *= radix
    return stages


def group_gather(block, axis):
    size = lax.axis_size(axis)
    position = lax.axis_index(axis)
    chunk = block[:, 0]
    depth = 0
    for radix, stride in reversed(radix_stages(size)):
        digit = (position // stride) % radix
        received = [chunk]
        for shift in range(1, radix):
            route = []
            for source in range(size):
                own = (source // stride) % radix
                route.append((source, source + (((own + shift) % radix) - own) * stride))
            received.append(lax.ppermute(chunk, axis, route))
        stacked = jnp.stack(received)
        ordered = [stacked[(digit - origin) % radix] for origin in range(radix)]
        chunk = jnp.stack(ordered, axis=1 + depth)
        depth += 1
    return chunk.reshape((chunk.shape[0], size) + chunk.shape[-2:])


def group_reduce(value, axis, combine):
    size = lax.axis_size(axis)
    position = lax.axis_index(axis)
    total = value
    for radix, stride in radix_stages(size):
        digit = (position // stride) % radix
        received = [total]
        for shift in range(1, radix):
            route = []
            for source in range(size):
                own = (source // stride) % radix
                route.append((source, source + (((own + shift) % radix) - own) * stride))
            received.append(lax.ppermute(total, axis, route))
        stacked = jnp.stack(received)
        ordered = [stacked[(digit - origin) % radix] for origin in range(radix)]
        total = ordered[0]
        for part in ordered[1:]:
            total = combine(total, part)
    return total


def from_behind(block, axis, distance):
    devices = range(lax.axis_size(axis))
    route = [(i - distance, i) for i in devices if i - distance in devices]
    return lax.ppermute(block, axis, route)


def block_mask(left_sizes, right_sizes, left_marks, right_marks, block_size):
    total = left_marks[:, None] + right_marks[None, :]
    allowed = (total == 4).astype(jnp.float32)
    offsets = jnp.arange(block_size, dtype=jnp.int32)
    live_rows = (offsets[None, :] < left_sizes[:, None]).astype(jnp.float32)
    live_cols = (offsets[None, :] < right_sizes[:, None]).astype(jnp.float32)
    return allowed[:, None, :, None] * live_rows[:, :, None, None] * live_cols[None, None, :, :]


def left_product(gathered):

    def product(rounded):
        return jnp.einsum(
            "wqac,qcrb->wqarb", gathered, rounded, preferred_element_type=jnp.float32
        ).astype(jnp.bfloat16)

    return product


def hamiltonian(product, right_block, pattern):

    def apply_all(vector):
        left_done = product(vector.astype(jnp.bfloat16))
        return (
            jnp.einsum(
                "wqarc,wrbc->qarb", left_done, right_block, preferred_element_type=jnp.float32
            )
            * pattern
        )

    return apply_all


def operator_bound(left_peak, right_peak, block_size):
    bound = jnp.sum((block_size * left_peak) * (block_size * right_peak))
    bound = jnp.minimum(bound, jnp.finfo(jnp.float32).max)
    return jnp.where(bound > 0, bound, 1.0)


def krylov(first, apply_all, bound):
    basis = [first, apply_all(first)]
    for step in range(ITERS):
        basis.append(apply_all(basis[-1]) / bound)
    count = len(basis)
    pairs = [(i, j) for i in range(count) for j in range(i, count)]
    partial = jnp.stack([jnp.sum(basis[i] * basis[j]) for i, j in pairs])
    gram_sums = group_reduce(partial, "blk", lambda a, b: a + b)
    rows = [[None] * count for _ in range(count)]
    for index, (i, j) in enumerate(pairs):
        rows[i][j] = gram_sums[index]
        rows[j][i] = gram_sums[index]
    gram = jnp.stack([jnp.stack(row) for row in rows])
    return basis, gram


def rotations(gram, bound):
    count = gram.shape[0]

    def inner(x, y):
        return jnp.sum(x[:, None] * gram * y[None, :])

    def shift(x):
        scaled = x[:-1] * jnp.concatenate([jnp.ones((1,), jnp.float32), jnp.full((count - 2,), bound)])
        return jnp.concatenate([jnp.zeros((1,), jnp.float32), scaled])

    unit = jnp.eye(count, dtype=jnp.float32)
    vector = unit[0]
    image = unit[1]
    ritz_value = inner(vector, image)
    for sweep in range(ITERS):
        residual = image - ritz_value * vector
        response = shift(residual)
        squared = inner(residual, residual) + EPS
        coupling = inner(residual, response) / squared
        midpoint = 0.5 * (ritz_value - coupling)
        radius = jnp.sqrt(midpoint * midpoint + squared)
        cosine = jnp.sqrt(0.5 * (1.0 - midpoint / radius))
        sine_value = -jnp.sqrt(0.5 * (1.0 + midpoint / radius))
        length = jnp.sqrt(squared)
        vector = cosine * vector + sine_value / length * residual
        image = cosine * image + sine_value / length * response
        ritz_value = 0.5 * (ritz_value + coupling) - radius
    return vector, ritz_value


def davidson(first, apply_all, bound):
    basis, gram = krylov(first, apply_all, bound)
    weights, ritz_value = rotations(gram, bound)
    vector = weights[0] * basis[0]
    for k in range(1, len(basis) - 1):
        vector = vector + weights[k] * basis[k]
    norm_sq = jnp.sum(weights[:, None] * gram * weights[None, :])
    return vector, ritz_value, norm_sq


def refresh(vector, product, states):
    rounded = vector.astype(jnp.bfloat16)
    left_done = product(rounded)
    return (
        states
        * jnp.einsum("qarb,wqarc->wrbc", rounded, left_done, preferred_element_type=jnp.float32)
    ).astype(jnp.bfloat16)


def peak(block):
    return jnp.max(jnp.abs(block.astype(jnp.float32)), axis=(1, 2, 3))


def local(guess, left_env, right_env, left_dims, right_dims, left_labels, right_labels):
    start_guess = guess[0].astype(jnp.float32)
    left_block = left_env[0]
    right_block = right_env[0]
    sector_count = start_guess.shape[0]
    block_size = start_guess.shape[1]
    owned_count = start_guess.shape[2]
    states = sector_count * block_size
    first_owned = lax.axis_index("blk") * owned_count
    owned_sizes = lax.dynamic_slice_in_dim(right_dims[0], first_owned, owned_count, 0)
    owned_marks = lax.dynamic_slice_in_dim(right_labels[0], first_owned, owned_count, 0)
    pattern = block_mask(left_dims[0], owned_sizes, left_labels[0], owned_marks, block_size)
    masked = start_guess * pattern
    early = group_reduce(
        jnp.concatenate([jnp.sum(masked * masked)[None], peak(right_block)]),
        "blk",
        lambda a, b: jnp.concatenate([a[:1] + b[:1], jnp.maximum(a[1:], b[1:])]),
    )
    right_peak = early[1:]
    first_gathered = group_gather(left_block, "blk")
    first_product = left_product(first_gathered)
    first_bound = operator_bound(peak(first_gathered), right_peak, block_size)
    first_start = masked / jnp.sqrt(early[0] + EPS)
    first_vector, first_energy, first_norm = davidson(
        first_start, hamiltonian(first_product, right_block, pattern), first_bound
    )
    fresh = refresh(first_vector, first_product, states)
    passed = from_behind(fresh, "sec", 1)
    second_left = jnp.where(lax.axis_index("sec") == 0, left_block, passed)
    second_gathered = group_gather(second_left, "blk")
    second_product = left_product(second_gathered)
    second_bound = operator_bound(peak(second_gathered), right_peak, block_size)
    second_start = first_vector * pattern / jnp.sqrt(first_norm + EPS)
    second_vector, second_energy, _ = davidson(
        second_start, hamiltonian(second_product, right_block, pattern), second_bound
    )
    waves = (states * second_vector)[None]
    energies = jnp.stack([first_energy, second_energy])[None]
    return (waves, energies)


def solution(mesh):
    return jax.shard_map(
        local,
        mesh=mesh,
        in_specs=(
            P("sec", None, None, "blk", None),
            P("sec", None, "blk", None, None),
            P("sec", None, "blk", None, None),
            P("sec", None),
            P("sec", None),
            P("sec", None),
            P("sec", None),
        ),
        out_specs=(P("sec", None, None, "blk", None), P("sec", None)),
        check_vma=False,
    )
```

```python
import jax
import jax.numpy as jnp
from jax import lax
from jax.sharding import PartitionSpec as P

ITERS = 2


EPS = 1e-06


def radix_stages(size):
    stages = []
    stride = 1
    for radix in (2, 4, 4, 2, 2, 2, 2):
        if stride >= size:
            break
        if size % (stride * radix):
            radix = 2
        stages.append((radix, stride))
        stride *= radix
    return stages


def group_gather(block, axis):
    size = lax.axis_size(axis)
    position = lax.axis_index(axis)
    chunk = block[:, 0]
    depth = 0
    for radix, stride in reversed(radix_stages(size)):
        digit = (position // stride) % radix
        received = [chunk]
        for shift in range(1, radix):
            route = []
            for source in range(size):
                own = (source // stride) % radix
                route.append((source, source + (((own + shift) % radix) - own) * stride))
            received.append(lax.ppermute(chunk, axis, route))
        stacked = jnp.stack(received)
        ordered = [stacked[(digit - origin) % radix] for origin in range(radix)]
        chunk = jnp.stack(ordered, axis=1 + depth)
        depth += 1
    return chunk


def group_reduce(value, axis, combine):
    size = lax.axis_size(axis)
    position = lax.axis_index(axis)
    total = value
    for radix, stride in radix_stages(size):
        digit = (position // stride) % radix
        received = [total]
        for shift in range(1, radix):
            route = []
            for source in range(size):
                own = (source // stride) % radix
                route.append((source, source + (((own + shift) % radix) - own) * stride))
            received.append(lax.ppermute(total, axis, route))
        stacked = jnp.stack(received)
        ordered = [stacked[(digit - origin) % radix] for origin in range(radix)]
        total = ordered[0]
        for part in ordered[1:]:
            total = combine(total, part)
    return total


def from_behind(block, axis, distance):
    devices = range(lax.axis_size(axis))
    route = [(i - distance, i) for i in devices if i - distance in devices]
    return lax.ppermute(block, axis, route)


def block_mask(left_sizes, right_sizes, left_marks, right_marks, block_size):
    total = left_marks[:, None] + right_marks[None, :]
    allowed = (total == 4).astype(jnp.float32)
    offsets = jnp.arange(block_size, dtype=jnp.int32)
    live_rows = (offsets[None, :] < left_sizes[:, None]).astype(jnp.float32)
    live_cols = (offsets[None, :] < right_sizes[:, None]).astype(jnp.float32)
    return allowed[:, None, :, None] * live_rows[:, :, None, None] * live_cols[None, None, :, :]


def left_product(gathered):
    digits = gathered.shape[1:-2]
    letters = "dghijklm"[: len(digits)]
    spec = "w" + letters + "ac," + letters + "crb->w" + letters + "arb"

    def product(rounded):
        split = rounded.reshape(digits + rounded.shape[1:])
        done = jnp.einsum(spec, gathered, split, preferred_element_type=jnp.float32)
        return done.reshape((done.shape[0], rounded.shape[0]) + done.shape[-3:]).astype(jnp.bfloat16)

    return product


def hamiltonian(product, right_block, pattern):

    def apply_all(vector):
        left_done = product(vector.astype(jnp.bfloat16))
        return (
            jnp.einsum(
                "wqarc,wrbc->qarb", left_done, right_block, preferred_element_type=jnp.float32
            )
            * pattern
        )

    return apply_all


def operator_bound(left_peak, right_peak, block_size):
    bound = jnp.sum((block_size * left_peak) * (block_size * right_peak))
    bound = jnp.minimum(bound, jnp.finfo(jnp.float32).max)
    return jnp.where(bound > 0, bound, 1.0)


def krylov(first, apply_all, bound):
    basis = [first, apply_all(first)]
    for step in range(ITERS):
        basis.append(apply_all(basis[-1]) / bound)
    count = len(basis)
    pairs = [(i, j) for i in range(count) for j in range(i, count)]
    partial = jnp.stack([jnp.sum(basis[i] * basis[j]) for i, j in pairs])
    gram_sums = group_reduce(partial, "blk", lambda a, b: a + b)
    gram = [[None] * count for _ in range(count)]
    for index, (i, j) in enumerate(pairs):
        gram[i][j] = gram_sums[index]
        gram[j][i] = gram_sums[index]
    return basis, gram


def inner(gram, x, y):
    total = None
    for i, left in enumerate(x):
        if left is None:
            continue
        for j, right in enumerate(y):
            if right is None:
                continue
            term = left * gram[i][j] * right
            total = term if total is None else total + term
    return total


def combine(a, x, b, y):
    out = []
    for left, right in zip(x, y):
        if left is None and right is None:
            out.append(None)
        elif right is None:
            out.append(a * left)
        elif left is None:
            out.append(b * right)
        else:
            out.append(a * left + b * right)
    return out


def rotations(gram, bound):
    count = len(gram)
    one = jnp.ones((), jnp.float32)
    vector = [one] + [None] * (count - 1)
    image = [None, one] + [None] * (count - 2)
    ritz_value = inner(gram, vector, image)
    for sweep in range(ITERS):
        residual = combine(one, image, -ritz_value, vector)
        response = [None, residual[0]] + [
            None if part is None else bound * part for part in residual[1:-1]
        ]
        squared = inner(gram, residual, residual) + EPS
        coupling = inner(gram, residual, response) / squared
        midpoint = 0.5 * (ritz_value - coupling)
        radius = jnp.sqrt(midpoint * midpoint + squared)
        cosine = jnp.sqrt(0.5 * (1.0 - midpoint / radius))
        sine_value = -jnp.sqrt(0.5 * (1.0 + midpoint / radius))
        length = jnp.sqrt(squared)
        vector = combine(cosine, vector, sine_value / length, residual)
        image = combine(cosine, image, sine_value / length, response)
        ritz_value = 0.5 * (ritz_value + coupling) - radius
    return vector, ritz_value


def davidson(first, apply_all, bound):
    basis, gram = krylov(first, apply_all, bound)
    weights, ritz_value = rotations(gram, bound)
    vector = None
    for weight, part in zip(weights, basis):
        if weight is None:
            continue
        vector = weight * part if vector is None else vector + weight * part
    norm_sq = inner(gram, weights, weights)
    return vector, ritz_value, norm_sq


def refresh(vector, product, states):
    rounded = vector.astype(jnp.bfloat16)
    left_done = product(rounded)
    return (
        states
        * jnp.einsum("qarb,wqarc->wrbc", rounded, left_done, preferred_element_type=jnp.float32)
    ).astype(jnp.bfloat16)


def peak(block):
    return jnp.max(jnp.abs(block.astype(jnp.float32)), axis=tuple(range(1, block.ndim)))


def local(guess, left_env, right_env, left_dims, right_dims, left_labels, right_labels):
    start_guess = guess[0].astype(jnp.float32)
    left_block = left_env[0]
    right_block = right_env[0]
    sector_count = start_guess.shape[0]
    block_size = start_guess.shape[1]
    owned_count = start_guess.shape[2]
    states = sector_count * block_size
    first_owned = lax.axis_index("blk") * owned_count
    owned_sizes = lax.dynamic_slice_in_dim(right_dims[0], first_owned, owned_count, 0)
    owned_marks = lax.dynamic_slice_in_dim(right_labels[0], first_owned, owned_count, 0)
    pattern = block_mask(left_dims[0], owned_sizes, left_labels[0], owned_marks, block_size)
    masked = start_guess * pattern
    early = group_reduce(
        jnp.concatenate([jnp.sum(masked * masked)[None], peak(right_block)]),
        "blk",
        lambda a, b: jnp.concatenate([a[:1] + b[:1], jnp.maximum(a[1:], b[1:])]),
    )
    right_peak = early[1:]
    first_gathered = group_gather(left_block, "blk")
    first_product = left_product(first_gathered)
    first_bound = operator_bound(peak(first_gathered), right_peak, block_size)
    first_start = masked / jnp.sqrt(early[0] + EPS)
    first_vector, first_energy, first_norm = davidson(
        first_start, hamiltonian(first_product, right_block, pattern), first_bound
    )
    fresh = refresh(first_vector, first_product, states)
    passed = from_behind(fresh, "sec", 1)
    second_left = jnp.where(lax.axis_index("sec") == 0, left_block, passed)
    second_gathered = group_gather(second_left, "blk")
    second_product = left_product(second_gathered)
    second_bound = operator_bound(peak(second_gathered), right_peak, block_size)
    second_start = first_vector * pattern / jnp.sqrt(first_norm + EPS)
    second_vector, second_energy, _ = davidson(
        second_start, hamiltonian(second_product, right_block, pattern), second_bound
    )
    waves = (states * second_vector)[None]
    energies = jnp.stack([first_energy, second_energy])[None]
    return (waves, energies)


def solution(mesh):
    return jax.shard_map(
        local,
        mesh=mesh,
        in_specs=(
            P("sec", None, None, "blk", None),
            P("sec", None, "blk", None, None),
            P("sec", None, "blk", None, None),
            P("sec", None),
            P("sec", None),
            P("sec", None),
            P("sec", None),
        ),
        out_specs=(P("sec", None, None, "blk", None), P("sec", None)),
        check_vma=False,
    )
```

```python
import jax
import jax.numpy as jnp
from jax import lax
from jax.sharding import PartitionSpec as P

ITERS = 2


EPS = 1e-06


def radix_stages(size):
    stages = []
    stride = 1
    for radix in (2, 4, 4, 2, 2, 2, 2):
        if stride >= size:
            break
        if size % (stride * radix):
            radix = 2
        stages.append((radix, stride))
        stride *= radix
    return stages


def group_gather(block, axis):
    size = lax.axis_size(axis)
    position = lax.axis_index(axis)
    chunk = block[:, 0]
    depth = 0
    for radix, stride in reversed(radix_stages(size)):
        digit = (position // stride) % radix
        received = [chunk]
        for shift in range(1, radix):
            route = []
            for source in range(size):
                own = (source // stride) % radix
                route.append((source, source + (((own + shift) % radix) - own) * stride))
            received.append(lax.ppermute(chunk, axis, route))
        stacked = jnp.stack(received)
        ordered = [stacked[(digit - origin) % radix] for origin in range(radix)]
        chunk = jnp.stack(ordered, axis=1 + depth)
        depth += 1
    return chunk


def group_reduce(value, axis, combine):
    size = lax.axis_size(axis)
    position = lax.axis_index(axis)
    total = value
    for radix, stride in radix_stages(size):
        digit = (position // stride) % radix
        received = [total]
        for shift in range(1, radix):
            route = []
            for source in range(size):
                own = (source // stride) % radix
                route.append((source, source + (((own + shift) % radix) - own) * stride))
            received.append(lax.ppermute(total, axis, route))
        stacked = jnp.stack(received)
        ordered = [stacked[(digit - origin) % radix] for origin in range(radix)]
        total = ordered[0]
        for part in ordered[1:]:
            total = combine(total, part)
    return total


def from_behind(block, axis, distance):
    devices = range(lax.axis_size(axis))
    route = [(i - distance, i) for i in devices if i - distance in devices]
    return lax.ppermute(block, axis, route)


def block_mask(left_sizes, right_sizes, left_marks, right_marks, block_size):
    total = left_marks[:, None] + right_marks[None, :]
    allowed = (total == 4).astype(jnp.float32)
    offsets = jnp.arange(block_size, dtype=jnp.int32)
    live_rows = (offsets[None, :] < left_sizes[:, None]).astype(jnp.float32)
    live_cols = (offsets[None, :] < right_sizes[:, None]).astype(jnp.float32)
    return allowed[:, None, :, None] * live_rows[:, :, None, None] * live_cols[None, None, :, :]


def left_product(gathered):
    digits = gathered.shape[1:-2]
    letters = "dghijklm"[: len(digits)]
    spec = "w" + letters + "ac," + letters + "crb->w" + letters + "arb"

    def product(rounded):
        split = rounded.reshape(digits + rounded.shape[1:])
        done = jnp.einsum(spec, gathered, split, preferred_element_type=jnp.float32)
        return done.reshape((done.shape[0], rounded.shape[0]) + done.shape[-3:]).astype(jnp.bfloat16)

    return product


def hamiltonian(product, right_block, pattern):

    def apply_all(vector):
        left_done = product(vector.astype(jnp.bfloat16))
        return (
            jnp.einsum(
                "wqarc,wrbc->qarb", left_done, right_block, preferred_element_type=jnp.float32
            )
            * pattern
        )

    return apply_all


def operator_bound(left_peak, right_peak, block_size):
    bound = jnp.sum((block_size * left_peak) * (block_size * right_peak))
    bound = jnp.minimum(bound, jnp.finfo(jnp.float32).max)
    return jnp.where(bound > 0, bound, 1.0)


def krylov(first, apply_all, bound):
    basis = [first, apply_all(first)]
    for step in range(ITERS):
        basis.append(apply_all(basis[-1]) / bound)
    count = len(basis)
    pairs = [(i, j) for i in range(count) for j in range(i, count)]
    partial = jnp.stack([jnp.sum(basis[i] * basis[j]) for i, j in pairs])
    gram_sums = group_reduce(partial, "blk", lambda a, b: a + b)
    gram = [[None] * count for _ in range(count)]
    for index, (i, j) in enumerate(pairs):
        gram[i][j] = gram_sums[index]
        gram[j][i] = gram_sums[index]
    return basis, gram


def inner(gram, x, y):
    total = None
    for i, left in enumerate(x):
        if left is None:
            continue
        for j, right in enumerate(y):
            if right is None:
                continue
            term = left * gram[i][j] * right
            total = term if total is None else total + term
    return total


def combine(a, x, b, y):
    out = []
    for left, right in zip(x, y):
        if left is None and right is None:
            out.append(None)
        elif right is None:
            out.append(a * left)
        elif left is None:
            out.append(b * right)
        else:
            out.append(a * left + b * right)
    return out


def rotations(gram, bound):
    count = len(gram)
    one = jnp.ones_like(bound)
    vector = [one] + [None] * (count - 1)
    image = [None, one] + [None] * (count - 2)
    ritz_value = inner(gram, vector, image)
    for sweep in range(ITERS):
        residual = combine(one, image, -ritz_value, vector)
        response = [None, residual[0]] + [
            None if part is None else bound * part for part in residual[1:-1]
        ]
        squared = inner(gram, residual, residual) + EPS
        coupling = inner(gram, residual, response) / squared
        midpoint = 0.5 * (ritz_value - coupling)
        radius = jnp.sqrt(midpoint * midpoint + squared)
        cosine = jnp.sqrt(0.5 * (1.0 - midpoint / radius))
        sine_value = -jnp.sqrt(0.5 * (1.0 + midpoint / radius))
        length = jnp.sqrt(squared)
        vector = combine(cosine, vector, sine_value / length, residual)
        image = combine(cosine, image, sine_value / length, response)
        ritz_value = 0.5 * (ritz_value + coupling) - radius
    return vector, ritz_value


def davidson(first, apply_all, bound, lane_zero):
    basis, gram = krylov(first, apply_all, bound)
    wide = [[entry + lane_zero for entry in row] for row in gram]
    weights, ritz_value = rotations(wide, bound + lane_zero)
    norm_sq = inner(wide, weights, weights)
    kept = [k for k, weight in enumerate(weights) if weight is not None]
    packed = lax.optimization_barrier(jnp.stack([weights[k] for k in kept] + [ritz_value, norm_sq]))
    scalars = packed[:, 0]
    vector = None
    for slot, k in enumerate(kept):
        term = scalars[slot] * basis[k]
        vector = term if vector is None else vector + term
    return vector, scalars[len(kept)], scalars[len(kept) + 1]


def refresh(vector, product, states):
    rounded = vector.astype(jnp.bfloat16)
    left_done = product(rounded)
    return (
        states
        * jnp.einsum("qarb,wqarc->wrbc", rounded, left_done, preferred_element_type=jnp.float32)
    ).astype(jnp.bfloat16)


def peak(block):
    return jnp.max(jnp.abs(block.astype(jnp.float32)), axis=tuple(range(1, block.ndim)))


def local(guess, left_env, right_env, left_dims, right_dims, left_labels, right_labels):
    start_guess = guess[0].astype(jnp.float32)
    left_block = left_env[0]
    right_block = right_env[0]
    sector_count = start_guess.shape[0]
    block_size = start_guess.shape[1]
    owned_count = start_guess.shape[2]
    states = sector_count * block_size
    first_owned = lax.axis_index("blk") * owned_count
    owned_sizes = lax.dynamic_slice_in_dim(right_dims[0], first_owned, owned_count, 0)
    owned_marks = lax.dynamic_slice_in_dim(right_labels[0], first_owned, owned_count, 0)
    pattern = block_mask(left_dims[0], owned_sizes, left_labels[0], owned_marks, block_size)
    masked = start_guess * pattern
    early = group_reduce(
        jnp.concatenate([jnp.sum(masked * masked)[None], peak(right_block)]),
        "blk",
        lambda a, b: jnp.concatenate([a[:1] + b[:1], jnp.maximum(a[1:], b[1:])]),
    )
    right_peak = early[1:]
    first_gathered = group_gather(left_block, "blk")
    first_product = left_product(first_gathered)
    first_bound = operator_bound(peak(first_gathered), right_peak, block_size)
    first_start = masked / jnp.sqrt(early[0] + EPS)
    lane_zero = pattern[0, 0, 0] * 0.0
    first_vector, first_energy, first_norm = davidson(
        first_start, hamiltonian(first_product, right_block, pattern), first_bound, lane_zero
    )
    fresh = refresh(first_vector, first_product, states)
    passed = from_behind(fresh, "sec", 1)
    second_left = jnp.where(lax.axis_index("sec") == 0, left_block, passed)
    second_gathered = group_gather(second_left, "blk")
    second_product = left_product(second_gathered)
    second_bound = operator_bound(peak(second_gathered), right_peak, block_size)
    second_start = first_vector * pattern / jnp.sqrt(first_norm + EPS)
    second_vector, second_energy, _ = davidson(
        second_start, hamiltonian(second_product, right_block, pattern), second_bound, lane_zero
    )
    waves = (states * second_vector)[None]
    energies = jnp.stack([first_energy, second_energy])[None]
    return (waves, energies)


def solution(mesh):
    return jax.shard_map(
        local,
        mesh=mesh,
        in_specs=(
            P("sec", None, None, "blk", None),
            P("sec", None, "blk", None, None),
            P("sec", None, "blk", None, None),
            P("sec", None),
            P("sec", None),
            P("sec", None),
            P("sec", None),
        ),
        out_specs=(P("sec", None, None, "blk", None), P("sec", None)),
        check_vma=False,
    )
```

```python
import jax
import jax.numpy as jnp
from jax import lax
from jax.sharding import PartitionSpec as P

ITERS = 2


EPS = 1e-06


def radix_stages(size):
    stages = []
    stride = 1
    for radix in (2, 4, 4, 2, 2, 2, 2):
        if stride >= size:
            break
        if size % (stride * radix):
            radix = 2
        stages.append((radix, stride))
        stride *= radix
    return stages


def group_gather(block, axis):
    size = lax.axis_size(axis)
    position = lax.axis_index(axis)
    chunk = block[:, 0]
    depth = 0
    for radix, stride in reversed(radix_stages(size)):
        digit = (position // stride) % radix
        received = [chunk]
        for shift in range(1, radix):
            route = []
            for source in range(size):
                own = (source // stride) % radix
                route.append((source, source + (((own + shift) % radix) - own) * stride))
            received.append(lax.ppermute(chunk, axis, route))
        stacked = jnp.stack(received)
        ordered = [stacked[(digit - origin) % radix] for origin in range(radix)]
        chunk = jnp.stack(ordered, axis=1 + depth)
        depth += 1
    return chunk


def group_reduce(value, axis, combine):
    size = lax.axis_size(axis)
    position = lax.axis_index(axis)
    total = value
    for radix, stride in radix_stages(size):
        digit = (position // stride) % radix
        received = [total]
        for shift in range(1, radix):
            route = []
            for source in range(size):
                own = (source // stride) % radix
                route.append((source, source + (((own + shift) % radix) - own) * stride))
            received.append(lax.ppermute(total, axis, route))
        stacked = jnp.stack(received)
        ordered = [stacked[(digit - origin) % radix] for origin in range(radix)]
        total = ordered[0]
        for part in ordered[1:]:
            total = combine(total, part)
    return total


def from_behind(block, axis, distance):
    devices = range(lax.axis_size(axis))
    route = [(i - distance, i) for i in devices if i - distance in devices]
    return lax.ppermute(block, axis, route)


def block_mask(left_sizes, right_sizes, left_marks, right_marks, block_size):
    total = left_marks[:, None] + right_marks[None, :]
    allowed = (total == 4).astype(jnp.float32)
    offsets = jnp.arange(block_size, dtype=jnp.int32)
    live_rows = (offsets[None, :] < left_sizes[:, None]).astype(jnp.float32)
    live_cols = (offsets[None, :] < right_sizes[:, None]).astype(jnp.float32)
    return allowed[:, None, :, None] * live_rows[:, :, None, None] * live_cols[None, None, :, :]


def left_product(gathered):
    digits = gathered.shape[1:-2]
    letters = "dghijklm"[: len(digits)]
    spec = "w" + letters + "ac," + letters + "crb->w" + letters + "arb"

    def product(rounded):
        split = rounded.reshape(digits + rounded.shape[1:])
        done = jnp.einsum(spec, gathered, split, preferred_element_type=jnp.float32)
        return done.reshape((done.shape[0], rounded.shape[0]) + done.shape[-3:]).astype(jnp.bfloat16)

    return product


def hamiltonian(product, right_block, pattern):

    def apply_all(vector):
        left_done = product(vector.astype(jnp.bfloat16))
        return (
            jnp.einsum(
                "wqarc,wrbc->qarb", left_done, right_block, preferred_element_type=jnp.float32
            )
            * pattern
        )

    return apply_all


def operator_bound(left_peak, right_peak, block_size):
    bound = jnp.sum((block_size * left_peak) * (block_size * right_peak))
    bound = jnp.minimum(bound, jnp.finfo(jnp.float32).max)
    return jnp.where(bound > 0, bound, 1.0)


def krylov(first, apply_all, bound):
    basis = [first, apply_all(first)]
    for step in range(ITERS):
        basis.append(apply_all(basis[-1]) / bound)
    count = len(basis)
    pairs = [(i, j) for i in range(count) for j in range(i, count)]
    partial = jnp.stack([jnp.sum(basis[i] * basis[j]) for i, j in pairs])
    gram_sums = group_reduce(partial, "blk", lambda a, b: a + b)
    gram = [[None] * count for _ in range(count)]
    for index, (i, j) in enumerate(pairs):
        gram[i][j] = gram_sums[index]
        gram[j][i] = gram_sums[index]
    return basis, gram


def inner(gram, x, y):
    total = None
    for i, left in enumerate(x):
        if left is None:
            continue
        for j, right in enumerate(y):
            if right is None:
                continue
            term = left * gram[i][j] * right
            total = term if total is None else total + term
    return total


def combine(a, x, b, y):
    out = []
    for left, right in zip(x, y):
        if left is None and right is None:
            out.append(None)
        elif right is None:
            out.append(a * left)
        elif left is None:
            out.append(b * right)
        else:
            out.append(a * left + b * right)
    return out


def rotations(gram, bound):
    count = len(gram)
    one = jnp.ones_like(bound)
    vector = [one] + [None] * (count - 1)
    image = [None, one] + [None] * (count - 2)
    ritz_value = inner(gram, vector, image)
    for sweep in range(ITERS):
        residual = combine(one, image, -ritz_value, vector)
        response = [None, residual[0]] + [
            None if part is None else bound * part for part in residual[1:-1]
        ]
        squared = inner(gram, residual, residual) + EPS
        correlation = inner(gram, residual, response)
        squared, correlation = lax.optimization_barrier((squared, correlation))
        coupling = correlation / squared
        midpoint = 0.5 * (ritz_value - coupling)
        radius = jnp.sqrt(midpoint * midpoint + squared)
        cosine = jnp.sqrt(0.5 * (1.0 - midpoint / radius))
        sine_value = -jnp.sqrt(0.5 * (1.0 + midpoint / radius))
        length = jnp.sqrt(squared)
        step = sine_value / length
        ritz_value = 0.5 * (ritz_value + coupling) - radius
        cosine, step, ritz_value = lax.optimization_barrier((cosine, step, ritz_value))
        vector = combine(cosine, vector, step, residual)
        image = combine(cosine, image, step, response)
        vector, image = lax.optimization_barrier((vector, image))
    return vector, ritz_value


def davidson(first, apply_all, bound, lane_zero):
    basis, gram = krylov(first, apply_all, bound)
    wide = [[entry + lane_zero for entry in row] for row in gram]
    weights, ritz_value = rotations(wide, bound + lane_zero)
    norm_sq = inner(wide, weights, weights)
    kept = [k for k, weight in enumerate(weights) if weight is not None]
    packed = lax.optimization_barrier(jnp.stack([weights[k] for k in kept] + [ritz_value, norm_sq]))
    scalars = packed[:, 0]
    vector = None
    for slot, k in enumerate(kept):
        term = scalars[slot] * basis[k]
        vector = term if vector is None else vector + term
    return vector, scalars[len(kept)], scalars[len(kept) + 1]


def refresh(vector, product, states):
    rounded = vector.astype(jnp.bfloat16)
    left_done = product(rounded)
    return (
        states
        * jnp.einsum("qarb,wqarc->wrbc", rounded, left_done, preferred_element_type=jnp.float32)
    ).astype(jnp.bfloat16)


def peak(block):
    return jnp.max(jnp.abs(block.astype(jnp.float32)), axis=tuple(range(1, block.ndim)))


def local(guess, left_env, right_env, left_dims, right_dims, left_labels, right_labels):
    start_guess = guess[0].astype(jnp.float32)
    left_block = left_env[0]
    right_block = right_env[0]
    sector_count = start_guess.shape[0]
    block_size = start_guess.shape[1]
    owned_count = start_guess.shape[2]
    states = sector_count * block_size
    first_owned = lax.axis_index("blk") * owned_count
    owned_sizes = lax.dynamic_slice_in_dim(right_dims[0], first_owned, owned_count, 0)
    owned_marks = lax.dynamic_slice_in_dim(right_labels[0], first_owned, owned_count, 0)
    pattern = block_mask(left_dims[0], owned_sizes, left_labels[0], owned_marks, block_size)
    masked = start_guess * pattern
    early = group_reduce(
        jnp.concatenate([jnp.sum(masked * masked)[None], peak(right_block)]),
        "blk",
        lambda a, b: jnp.concatenate([a[:1] + b[:1], jnp.maximum(a[1:], b[1:])]),
    )
    right_peak = early[1:]
    first_gathered = group_gather(left_block, "blk")
    first_product = left_product(first_gathered)
    first_bound = operator_bound(peak(first_gathered), right_peak, block_size)
    first_start = masked / jnp.sqrt(early[0] + EPS)
    lane_zero = pattern[0, 0, 0] * 0.0
    first_vector, first_energy, first_norm = davidson(
        first_start, hamiltonian(first_product, right_block, pattern), first_bound, lane_zero
    )
    fresh = refresh(first_vector, first_product, states)
    passed = from_behind(fresh, "sec", 1)
    second_left = jnp.where(lax.axis_index("sec") == 0, left_block, passed)
    second_gathered = group_gather(second_left, "blk")
    second_product = left_product(second_gathered)
    second_bound = operator_bound(peak(second_gathered), right_peak, block_size)
    second_start = first_vector * pattern / jnp.sqrt(first_norm + EPS)
    second_vector, second_energy, _ = davidson(
        second_start, hamiltonian(second_product, right_block, pattern), second_bound, lane_zero
    )
    waves = (states * second_vector)[None]
    energies = jnp.stack([first_energy, second_energy])[None]
    return (waves, energies)


def solution(mesh):
    return jax.shard_map(
        local,
        mesh=mesh,
        in_specs=(
            P("sec", None, None, "blk", None),
            P("sec", None, "blk", None, None),
            P("sec", None, "blk", None, None),
            P("sec", None),
            P("sec", None),
            P("sec", None),
            P("sec", None),
        ),
        out_specs=(P("sec", None, None, "blk", None), P("sec", None)),
        check_vma=False,
    )
```

```python
import jax
import jax.numpy as jnp
from jax import lax
from jax.sharding import PartitionSpec as P

ITERS = 2


EPS = 1e-06


def radix_stages(size):
    stages = []
    stride = 1
    for radix in (2, 4, 4, 2, 2, 2, 2):
        if stride >= size:
            break
        if size % (stride * radix):
            radix = 2
        stages.append((radix, stride))
        stride *= radix
    return stages


def group_gather(block, axis):
    size = lax.axis_size(axis)
    position = lax.axis_index(axis)
    chunk = block[:, 0]
    depth = 0
    for radix, stride in reversed(radix_stages(size)):
        digit = (position // stride) % radix
        received = [chunk]
        for shift in range(1, radix):
            route = []
            for source in range(size):
                own = (source // stride) % radix
                route.append((source, source + (((own + shift) % radix) - own) * stride))
            received.append(lax.ppermute(chunk, axis, route))
        stacked = jnp.stack(received)
        ordered = [stacked[(digit - origin) % radix] for origin in range(radix)]
        chunk = jnp.stack(ordered, axis=1 + depth)
        if depth == 0:
            first_stage = chunk
        depth += 1
    return chunk, first_stage


def group_reduce(value, axis, combine):
    size = lax.axis_size(axis)
    position = lax.axis_index(axis)
    total = value
    for radix, stride in radix_stages(size):
        digit = (position // stride) % radix
        received = [total]
        for shift in range(1, radix):
            route = []
            for source in range(size):
                own = (source // stride) % radix
                route.append((source, source + (((own + shift) % radix) - own) * stride))
            received.append(lax.ppermute(total, axis, route))
        stacked = jnp.stack(received)
        ordered = [stacked[(digit - origin) % radix] for origin in range(radix)]
        total = ordered[0]
        for part in ordered[1:]:
            total = combine(total, part)
    return total


def from_behind(block, axis, distance):
    devices = range(lax.axis_size(axis))
    route = [(i - distance, i) for i in devices if i - distance in devices]
    return lax.ppermute(block, axis, route)


def block_mask(left_sizes, right_sizes, left_marks, right_marks, block_size):
    total = left_marks[:, None] + right_marks[None, :]
    allowed = (total == 4).astype(jnp.float32)
    offsets = jnp.arange(block_size, dtype=jnp.int32)
    live_rows = (offsets[None, :] < left_sizes[:, None]).astype(jnp.float32)
    live_cols = (offsets[None, :] < right_sizes[:, None]).astype(jnp.float32)
    return allowed[:, None, :, None] * live_rows[:, :, None, None] * live_cols[None, None, :, :]


def left_product(gathered):
    digits = gathered.shape[1:-2]
    letters = "dghijklm"[: len(digits)]
    spec = "w" + letters + "ac," + letters + "crb->w" + letters + "arb"

    def product(rounded):
        split = rounded.reshape(digits + rounded.shape[1:])
        done = jnp.einsum(spec, gathered, split, preferred_element_type=jnp.float32)
        return done.reshape((done.shape[0], rounded.shape[0]) + done.shape[-3:]).astype(jnp.bfloat16)

    return product


def hamiltonian(product, right_block, pattern):

    def apply_all(vector):
        left_done = product(vector.astype(jnp.bfloat16))
        return (
            jnp.einsum(
                "wqarc,wrbc->qarb", left_done, right_block, preferred_element_type=jnp.float32
            )
            * pattern
        )

    return apply_all


def operator_bound(left_peak, right_peak, block_size):
    bound = jnp.sum((block_size * left_peak) * (block_size * right_peak))
    bound = jnp.minimum(bound, jnp.finfo(jnp.float32).max)
    return jnp.where(bound > 0, bound, 1.0)


def krylov(first, apply_all, bound):
    basis = [first, apply_all(first)]
    for step in range(ITERS):
        basis.append(apply_all(basis[-1]) / bound)
    count = len(basis)
    pairs = [(i, j) for i in range(count) for j in range(i, count)]
    partial = jnp.stack([jnp.sum(basis[i] * basis[j]) for i, j in pairs])
    gram_sums = group_reduce(partial, "blk", lambda a, b: a + b)
    gram = [[None] * count for _ in range(count)]
    for index, (i, j) in enumerate(pairs):
        gram[i][j] = gram_sums[index]
        gram[j][i] = gram_sums[index]
    return basis, gram


def inner(gram, x, y):
    total = None
    for i, left in enumerate(x):
        if left is None:
            continue
        for j, right in enumerate(y):
            if right is None:
                continue
            term = left * gram[i][j] * right
            total = term if total is None else total + term
    return total


def combine(a, x, b, y):
    out = []
    for left, right in zip(x, y):
        if left is None and right is None:
            out.append(None)
        elif right is None:
            out.append(a * left)
        elif left is None:
            out.append(b * right)
        else:
            out.append(a * left + b * right)
    return out


def rotations(gram, bound):
    count = len(gram)
    one = jnp.ones((), jnp.float32)
    vector = [one] + [None] * (count - 1)
    image = [None, one] + [None] * (count - 2)
    ritz_value = inner(gram, vector, image)
    for sweep in range(ITERS):
        residual = combine(one, image, -ritz_value, vector)
        response = [None, residual[0]] + [
            None if part is None else bound * part for part in residual[1:-1]
        ]
        squared = inner(gram, residual, residual) + EPS
        coupling = inner(gram, residual, response) / squared
        midpoint = 0.5 * (ritz_value - coupling)
        radius = jnp.sqrt(midpoint * midpoint + squared)
        cosine = jnp.sqrt(0.5 * (1.0 - midpoint / radius))
        sine_value = -jnp.sqrt(0.5 * (1.0 + midpoint / radius))
        length = jnp.sqrt(squared)
        vector = combine(cosine, vector, sine_value / length, residual)
        image = combine(cosine, image, sine_value / length, response)
        ritz_value = 0.5 * (ritz_value + coupling) - radius
    return vector, ritz_value


def davidson(first, apply_all, bound):
    basis, gram = krylov(first, apply_all, bound)
    weights, ritz_value = rotations(gram, bound)
    vector = None
    for weight, part in zip(weights, basis):
        if weight is None:
            continue
        vector = weight * part if vector is None else vector + weight * part
    norm_sq = inner(gram, weights, weights)
    return vector, ritz_value, norm_sq


def refresh(vector, product, states):
    rounded = vector.astype(jnp.bfloat16)
    left_done = product(rounded)
    return (
        states
        * jnp.einsum("qarb,wqarc->wrbc", rounded, left_done, preferred_element_type=jnp.float32)
    ).astype(jnp.bfloat16)


def peak(block):
    return jnp.max(jnp.abs(block.astype(jnp.float32)), axis=tuple(range(1, block.ndim)))


def local(guess, left_env, right_env, left_dims, right_dims, left_labels, right_labels):
    start_guess = guess[0].astype(jnp.float32)
    left_block = left_env[0]
    right_block = right_env[0]
    sector_count = start_guess.shape[0]
    block_size = start_guess.shape[1]
    owned_count = start_guess.shape[2]
    states = sector_count * block_size
    first_owned = lax.axis_index("blk") * owned_count
    owned_sizes = lax.dynamic_slice_in_dim(right_dims[0], first_owned, owned_count, 0)
    owned_marks = lax.dynamic_slice_in_dim(right_labels[0], first_owned, owned_count, 0)
    pattern = block_mask(left_dims[0], owned_sizes, left_labels[0], owned_marks, block_size)
    masked = start_guess * pattern
    first_gathered, first_stage = group_gather(left_block, "blk")
    after_stage = first_stage[0, 0, 0, 0].astype(jnp.float32) * 0.0
    early = group_reduce(
        jnp.concatenate([jnp.sum(masked * masked)[None], peak(right_block)]) + after_stage,
        "blk",
        lambda a, b: jnp.concatenate([a[:1] + b[:1], jnp.maximum(a[1:], b[1:])]),
    )
    right_peak = early[1:]
    first_product = left_product(first_gathered)
    first_bound = operator_bound(peak(first_gathered), right_peak, block_size)
    first_start = masked / jnp.sqrt(early[0] + EPS)
    first_vector, first_energy, first_norm = davidson(
        first_start, hamiltonian(first_product, right_block, pattern), first_bound
    )
    fresh = refresh(first_vector, first_product, states)
    passed = from_behind(fresh, "sec", 1)
    second_left = jnp.where(lax.axis_index("sec") == 0, left_block, passed)
    second_gathered, _ = group_gather(second_left, "blk")
    second_product = left_product(second_gathered)
    second_bound = operator_bound(peak(second_gathered), right_peak, block_size)
    second_start = first_vector * pattern / jnp.sqrt(first_norm + EPS)
    second_vector, second_energy, _ = davidson(
        second_start, hamiltonian(second_product, right_block, pattern), second_bound
    )
    waves = (states * second_vector)[None]
    energies = jnp.stack([first_energy, second_energy])[None]
    return (waves, energies)


def solution(mesh):
    return jax.shard_map(
        local,
        mesh=mesh,
        in_specs=(
            P("sec", None, None, "blk", None),
            P("sec", None, "blk", None, None),
            P("sec", None, "blk", None, None),
            P("sec", None),
            P("sec", None),
            P("sec", None),
            P("sec", None),
        ),
        out_specs=(P("sec", None, None, "blk", None), P("sec", None)),
        check_vma=False,
    )
```

```python
import jax
import jax.numpy as jnp
from jax import lax
from jax.sharding import PartitionSpec as P

ITERS = 2


EPS = 1e-06


def radix_stages(size):
    stages = []
    stride = 1
    for radix in (2, 4, 4, 2, 2, 2, 2):
        if stride >= size:
            break
        if size % (stride * radix):
            radix = 2
        stages.append((radix, stride))
        stride *= radix
    return stages


def group_gather(block, axis):
    size = lax.axis_size(axis)
    position = lax.axis_index(axis)
    chunk = block[:, 0]
    depth = 0
    for radix, stride in reversed(radix_stages(size)):
        digit = (position // stride) % radix
        received = [chunk]
        for shift in range(1, radix):
            route = []
            for source in range(size):
                own = (source // stride) % radix
                route.append((source, source + (((own + shift) % radix) - own) * stride))
            received.append(lax.ppermute(chunk, axis, route))
        stacked = jnp.stack(received)
        ordered = [stacked[(digit - origin) % radix] for origin in range(radix)]
        chunk = jnp.stack(ordered, axis=1 + depth)
        if depth == 0:
            first_stage = chunk
        depth += 1
    return chunk, first_stage


def group_reduce(value, axis, combine):
    size = lax.axis_size(axis)
    total = value
    for radix, stride in radix_stages(size):
        received = [total]
        for shift in range(1, radix):
            route = []
            for source in range(size):
                own = (source // stride) % radix
                route.append((source, source + ((own ^ shift) - own) * stride))
            received.append(lax.ppermute(total, axis, route))
        while len(received) > 1:
            received = [combine(received[k], received[k + 1]) for k in range(0, len(received), 2)]
        total = received[0]
    return total


def from_behind(block, axis, distance):
    devices = range(lax.axis_size(axis))
    route = [(i - distance, i) for i in devices if i - distance in devices]
    return lax.ppermute(block, axis, route)


def block_mask(left_sizes, right_sizes, left_marks, right_marks, block_size):
    total = left_marks[:, None] + right_marks[None, :]
    allowed = (total == 4).astype(jnp.float32)
    offsets = jnp.arange(block_size, dtype=jnp.int32)
    live_rows = (offsets[None, :] < left_sizes[:, None]).astype(jnp.float32)
    live_cols = (offsets[None, :] < right_sizes[:, None]).astype(jnp.float32)
    return allowed[:, None, :, None] * live_rows[:, :, None, None] * live_cols[None, None, :, :]


def left_product(gathered):
    digits = gathered.shape[1:-2]
    letters = "dghijklm"[: len(digits)]
    spec = "w" + letters + "ac," + letters + "crb->w" + letters + "arb"

    def product(rounded):
        split = rounded.reshape(digits + rounded.shape[1:])
        done = jnp.einsum(spec, gathered, split, preferred_element_type=jnp.float32)
        return done.reshape((done.shape[0], rounded.shape[0]) + done.shape[-3:]).astype(jnp.bfloat16)

    return product


def hamiltonian(product, right_block, pattern):

    def apply_all(vector):
        left_done = product(vector.astype(jnp.bfloat16))
        return (
            jnp.einsum(
                "wqarc,wrbc->qarb", left_done, right_block, preferred_element_type=jnp.float32
            )
            * pattern
        )

    return apply_all


def operator_bound(left_peak, right_peak, block_size):
    bound = jnp.sum((block_size * left_peak) * (block_size * right_peak))
    bound = jnp.minimum(bound, jnp.finfo(jnp.float32).max)
    return jnp.where(bound > 0, bound, 1.0)


def krylov(first, apply_all, bound):
    basis = [first, apply_all(first)]
    for step in range(ITERS):
        basis.append(apply_all(basis[-1]) / bound)
    count = len(basis)
    pairs = [(i, j) for i in range(count) for j in range(i, count)]
    partial = jnp.stack([jnp.sum(basis[i] * basis[j]) for i, j in pairs])
    gram_sums = group_reduce(partial, "blk", lambda a, b: a + b)
    gram = [[None] * count for _ in range(count)]
    for index, (i, j) in enumerate(pairs):
        gram[i][j] = gram_sums[index]
        gram[j][i] = gram_sums[index]
    return basis, gram


def inner(gram, x, y):
    total = None
    for i, left in enumerate(x):
        if left is None:
            continue
        for j, right in enumerate(y):
            if right is None:
                continue
            term = left * gram[i][j] * right
            total = term if total is None else total + term
    return total


def combine(a, x, b, y):
    out = []
    for left, right in zip(x, y):
        if left is None and right is None:
            out.append(None)
        elif right is None:
            out.append(a * left)
        elif left is None:
            out.append(b * right)
        else:
            out.append(a * left + b * right)
    return out


def rotations(gram, bound):
    count = len(gram)
    one = jnp.ones((), jnp.float32)
    vector = [one] + [None] * (count - 1)
    image = [None, one] + [None] * (count - 2)
    ritz_value = inner(gram, vector, image)
    for sweep in range(ITERS):
        residual = combine(one, image, -ritz_value, vector)
        response = [None, residual[0]] + [
            None if part is None else bound * part for part in residual[1:-1]
        ]
        squared = inner(gram, residual, residual) + EPS
        coupling = inner(gram, residual, response) / squared
        midpoint = 0.5 * (ritz_value - coupling)
        radius = jnp.sqrt(midpoint * midpoint + squared)
        cosine = jnp.sqrt(0.5 * (1.0 - midpoint / radius))
        sine_value = -jnp.sqrt(0.5 * (1.0 + midpoint / radius))
        length = jnp.sqrt(squared)
        vector = combine(cosine, vector, sine_value / length, residual)
        image = combine(cosine, image, sine_value / length, response)
        ritz_value = 0.5 * (ritz_value + coupling) - radius
    return vector, ritz_value


def davidson(first, apply_all, bound):
    basis, gram = krylov(first, apply_all, bound)
    weights, ritz_value = rotations(gram, bound)
    vector = None
    for weight, part in zip(weights, basis):
        if weight is None:
            continue
        vector = weight * part if vector is None else vector + weight * part
    norm_sq = inner(gram, weights, weights)
    return vector, ritz_value, norm_sq


def refresh(vector, product, states):
    rounded = vector.astype(jnp.bfloat16)
    left_done = product(rounded)
    return (
        states
        * jnp.einsum("qarb,wqarc->wrbc", rounded, left_done, preferred_element_type=jnp.float32)
    ).astype(jnp.bfloat16)


def peak(block):
    return jnp.max(jnp.abs(block.astype(jnp.float32)), axis=tuple(range(1, block.ndim)))


def local(guess, left_env, right_env, left_dims, right_dims, left_labels, right_labels):
    start_guess = guess[0].astype(jnp.float32)
    left_block = left_env[0]
    right_block = right_env[0]
    sector_count = start_guess.shape[0]
    block_size = start_guess.shape[1]
    owned_count = start_guess.shape[2]
    states = sector_count * block_size
    first_owned = lax.axis_index("blk") * owned_count
    owned_sizes = lax.dynamic_slice_in_dim(right_dims[0], first_owned, owned_count, 0)
    owned_marks = lax.dynamic_slice_in_dim(right_labels[0], first_owned, owned_count, 0)
    pattern = block_mask(left_dims[0], owned_sizes, left_labels[0], owned_marks, block_size)
    masked = start_guess * pattern
    first_gathered, first_stage = group_gather(left_block, "blk")
    after_stage = first_stage[0, 0, 0, 0].astype(jnp.float32) * 0.0
    early = group_reduce(
        jnp.concatenate([jnp.sum(masked * masked)[None], peak(right_block)]) + after_stage,
        "blk",
        lambda a, b: jnp.concatenate([a[:1] + b[:1], jnp.maximum(a[1:], b[1:])]),
    )
    right_peak = early[1:]
    first_product = left_product(first_gathered)
    first_bound = operator_bound(peak(first_gathered), right_peak, block_size)
    first_start = masked / jnp.sqrt(early[0] + EPS)
    first_vector, first_energy, first_norm = davidson(
        first_start, hamiltonian(first_product, right_block, pattern), first_bound
    )
    fresh = refresh(first_vector, first_product, states)
    passed = from_behind(fresh, "sec", 1)
    second_left = jnp.where(lax.axis_index("sec") == 0, left_block, passed)
    second_gathered, _ = group_gather(second_left, "blk")
    second_product = left_product(second_gathered)
    second_bound = operator_bound(peak(second_gathered), right_peak, block_size)
    second_start = first_vector * pattern / jnp.sqrt(first_norm + EPS)
    second_vector, second_energy, _ = davidson(
        second_start, hamiltonian(second_product, right_block, pattern), second_bound
    )
    waves = (states * second_vector)[None]
    energies = jnp.stack([first_energy, second_energy])[None]
    return (waves, energies)


def solution(mesh):
    return jax.shard_map(
        local,
        mesh=mesh,
        in_specs=(
            P("sec", None, None, "blk", None),
            P("sec", None, "blk", None, None),
            P("sec", None, "blk", None, None),
            P("sec", None),
            P("sec", None),
            P("sec", None),
            P("sec", None),
        ),
        out_specs=(P("sec", None, None, "blk", None), P("sec", None)),
        check_vma=False,
    )
```

```python
import math

import jax
import jax.numpy as jnp
from jax import lax
from jax.sharding import PartitionSpec as P

ITERS = 2


EPS = 1e-06


def radix_stages(size):
    stages = []
    stride = 1
    for radix in (2, 4, 4, 2, 2, 2, 2):
        if stride >= size:
            break
        if size % (stride * radix):
            radix = 2
        stages.append((radix, stride))
        stride *= radix
    return stages


def group_gather(block, axis):
    size = lax.axis_size(axis)
    position = lax.axis_index(axis)
    chunk = block[:, 0]
    depth = 0
    for radix, stride in reversed(radix_stages(size)):
        digit = (position // stride) % radix
        received = [chunk]
        for shift in range(1, radix):
            route = []
            for source in range(size):
                own = (source // stride) % radix
                route.append((source, source + (((own + shift) % radix) - own) * stride))
            received.append(lax.ppermute(chunk, axis, route))
        stacked = jnp.stack(received)
        ordered = [stacked[(digit - origin) % radix] for origin in range(radix)]
        chunk = jnp.stack(ordered, axis=1 + depth)
        if depth == 0:
            first_stage = chunk
        depth += 1
    return chunk, first_stage


def group_reduce(value, axis, combine):
    size = lax.axis_size(axis)
    position = lax.axis_index(axis)
    total = value
    for radix, stride in radix_stages(size):
        digit = (position // stride) % radix
        received = [total]
        for shift in range(1, radix):
            route = []
            for source in range(size):
                own = (source // stride) % radix
                route.append((source, source + (((own + shift) % radix) - own) * stride))
            received.append(lax.ppermute(total, axis, route))
        stacked = jnp.stack(received)
        ordered = [stacked[(digit - origin) % radix] for origin in range(radix)]
        total = ordered[0]
        for part in ordered[1:]:
            total = combine(total, part)
    return total


def from_behind(block, axis, distance):
    devices = range(lax.axis_size(axis))
    route = [(i - distance, i) for i in devices if i - distance in devices]
    return lax.ppermute(block, axis, route)


def block_mask(left_sizes, right_sizes, left_marks, right_marks, block_size):
    total = left_marks[:, None] + right_marks[None, :]
    allowed = (total == 4).astype(jnp.float32)
    offsets = jnp.arange(block_size, dtype=jnp.int32)
    live_rows = (offsets[None, :] < left_sizes[:, None]).astype(jnp.float32)
    live_cols = (offsets[None, :] < right_sizes[:, None]).astype(jnp.float32)
    return allowed[:, None, :, None] * live_rows[:, :, None, None] * live_cols[None, None, :, :]


def left_product(gathered):
    digits = gathered.shape[1:-2]
    letters = "dghijklm"[: len(digits)]
    spec = "w" + letters + "ac," + letters + "crb->w" + letters + "arb"

    def product(rounded):
        split = rounded.reshape(digits + rounded.shape[1:])
        done = jnp.einsum(spec, gathered, split, preferred_element_type=jnp.float32)
        return done.reshape((done.shape[0], rounded.shape[0]) + done.shape[-3:]).astype(jnp.bfloat16)

    return product


def hamiltonian(product, right_block, pattern):

    def apply_all(vector):
        left_done = product(vector.astype(jnp.bfloat16))
        return (
            jnp.einsum(
                "wqarc,wrbc->qarb", left_done, right_block, preferred_element_type=jnp.float32
            )
            * pattern
        )

    return apply_all


def right_first(gathered, right_block, pattern):
    digits = gathered.shape[1:-2]
    letters = "dghijklm"[: len(digits)]
    spec = "w" + letters + "ac,w" + letters + "crb->" + letters + "arb"

    def partial(vector):
        return jnp.einsum(
            "qcrd,wrbd->wqcrb", vector.astype(jnp.bfloat16), right_block,
            preferred_element_type=jnp.float32,
        ).astype(jnp.bfloat16)

    def finish(done):
        split = done.reshape((done.shape[0],) + digits + done.shape[2:])
        out = jnp.einsum(spec, gathered, split, preferred_element_type=jnp.float32)
        return out.reshape((done.shape[1],) + out.shape[-3:]) * pattern

    return partial, finish


def operator_bound(left_peak, right_peak, block_size):
    bound = jnp.sum((block_size * left_peak) * (block_size * right_peak))
    bound = jnp.minimum(bound, jnp.finfo(jnp.float32).max)
    return jnp.where(bound > 0, bound, 1.0)


def krylov(first, image, apply_all, bound):
    basis = [first, image]
    for step in range(ITERS):
        basis.append(apply_all(basis[-1]) / bound)
    count = len(basis)
    pairs = [(i, j) for i in range(count) for j in range(i, count)]
    partial = jnp.stack([jnp.sum(basis[i] * basis[j]) for i, j in pairs])
    gram_sums = group_reduce(partial, "blk", lambda a, b: a + b)
    gram = [[None] * count for _ in range(count)]
    for index, (i, j) in enumerate(pairs):
        gram[i][j] = gram_sums[index]
        gram[j][i] = gram_sums[index]
    return basis, gram


def inner(gram, x, y):
    total = None
    for i, left in enumerate(x):
        if left is None:
            continue
        for j, right in enumerate(y):
            if right is None:
                continue
            term = left * gram[i][j] * right
            total = term if total is None else total + term
    return total


def combine(a, x, b, y):
    out = []
    for left, right in zip(x, y):
        if left is None and right is None:
            out.append(None)
        elif right is None:
            out.append(a * left)
        elif left is None:
            out.append(b * right)
        else:
            out.append(a * left + b * right)
    return out


def rotations(gram, bound):
    count = len(gram)
    one = jnp.ones((), jnp.float32)
    vector = [one] + [None] * (count - 1)
    image = [None, one] + [None] * (count - 2)
    ritz_value = inner(gram, vector, image)
    for sweep in range(ITERS):
        residual = combine(one, image, -ritz_value, vector)
        response = [None, residual[0]] + [
            None if part is None else bound * part for part in residual[1:-1]
        ]
        squared = inner(gram, residual, residual) + EPS
        coupling = inner(gram, residual, response) / squared
        midpoint = 0.5 * (ritz_value - coupling)
        radius = jnp.sqrt(midpoint * midpoint + squared)
        cosine = jnp.sqrt(0.5 * (1.0 - midpoint / radius))
        sine_value = -jnp.sqrt(0.5 * (1.0 + midpoint / radius))
        length = jnp.sqrt(squared)
        vector = combine(cosine, vector, sine_value / length, residual)
        image = combine(cosine, image, sine_value / length, response)
        ritz_value = 0.5 * (ritz_value + coupling) - radius
    return vector, ritz_value


def davidson(first, image, apply_all, bound):
    basis, gram = krylov(first, image, apply_all, bound)
    weights, ritz_value = rotations(gram, bound)
    vector = None
    for weight, part in zip(weights, basis):
        if weight is None:
            continue
        vector = weight * part if vector is None else vector + weight * part
    norm_sq = inner(gram, weights, weights)
    return vector, ritz_value, norm_sq


def refresh(vector, product, states):
    rounded = vector.astype(jnp.bfloat16)
    left_done = product(rounded)
    return (
        states
        * jnp.einsum("qarb,wqarc->wrbc", rounded, left_done, preferred_element_type=jnp.float32)
    ).astype(jnp.bfloat16)


def peak(block):
    return jnp.max(jnp.abs(block.astype(jnp.float32)), axis=tuple(range(1, block.ndim)))


def local(guess, left_env, right_env, left_dims, right_dims, left_labels, right_labels):
    start_guess = guess[0].astype(jnp.float32)
    left_block = left_env[0]
    right_block = right_env[0]
    sector_count = start_guess.shape[0]
    block_size = start_guess.shape[1]
    owned_count = start_guess.shape[2]
    states = sector_count * block_size
    first_owned = lax.axis_index("blk") * owned_count
    owned_sizes = lax.dynamic_slice_in_dim(right_dims[0], first_owned, owned_count, 0)
    owned_marks = lax.dynamic_slice_in_dim(right_labels[0], first_owned, owned_count, 0)
    pattern = block_mask(left_dims[0], owned_sizes, left_labels[0], owned_marks, block_size)
    masked = start_guess * pattern
    first_gathered, first_stage = group_gather(left_block, "blk")
    after_stage = first_stage[0, 0, 0, 0].astype(jnp.float32) * 0.0
    early = group_reduce(
        jnp.concatenate([jnp.sum(masked * masked)[None], peak(right_block)]) + after_stage,
        "blk",
        lambda a, b: jnp.concatenate([a[:1] + b[:1], jnp.maximum(a[1:], b[1:])]),
    )
    right_peak = early[1:]
    first_product = left_product(first_gathered)
    first_bound = operator_bound(peak(first_gathered), right_peak, block_size)
    first_scale = jnp.sqrt(early[0] + EPS)
    first_start = masked / first_scale
    first_partial, first_finish = right_first(first_gathered, right_block, pattern)
    cells = 1
    for extent in guess.shape[1:]:
        cells *= extent
    shrink = 2.0 ** -math.ceil(math.log2(6.0 * math.sqrt(cells * lax.axis_size("blk"))))
    first_image = first_finish(first_partial(masked * shrink)) / (first_scale * shrink)
    first_vector, first_energy, first_norm = davidson(
        first_start, first_image, hamiltonian(first_product, right_block, pattern), first_bound
    )
    fresh = refresh(first_vector, first_product, states)
    passed = from_behind(fresh, "sec", 1)
    second_left = jnp.where(lax.axis_index("sec") == 0, left_block, passed)
    second_start = first_vector * pattern / jnp.sqrt(first_norm + EPS)
    second_half = jnp.einsum(
        "qcrd,wrbd->wqcrb", second_start.astype(jnp.bfloat16), right_block,
        preferred_element_type=jnp.float32,
    ).astype(jnp.bfloat16)
    second_gathered, _ = group_gather(second_left, "blk")
    second_product = left_product(second_gathered)
    second_bound = operator_bound(peak(second_gathered), right_peak, block_size)
    _, second_finish = right_first(second_gathered, right_block, pattern)
    second_vector, second_energy, _ = davidson(
        second_start, second_finish(second_half), hamiltonian(second_product, right_block, pattern), second_bound
    )
    waves = (states * second_vector)[None]
    energies = jnp.stack([first_energy, second_energy])[None]
    return (waves, energies)


def solution(mesh):
    return jax.shard_map(
        local,
        mesh=mesh,
        in_specs=(
            P("sec", None, None, "blk", None),
            P("sec", None, "blk", None, None),
            P("sec", None, "blk", None, None),
            P("sec", None),
            P("sec", None),
            P("sec", None),
            P("sec", None),
        ),
        out_specs=(P("sec", None, None, "blk", None), P("sec", None)),
        check_vma=False,
    )
```

```python
import jax
import jax.numpy as jnp
from jax import lax
from jax.sharding import PartitionSpec as P

ITERS = 2


EPS = 1e-06


def radix_stages(size):
    stages = []
    stride = 1
    for radix in (2, 4, 4, 2, 2, 2, 2):
        if stride >= size:
            break
        if size % (stride * radix):
            radix = 2
        stages.append((radix, stride))
        stride *= radix
    return stages


def group_gather(block, axis):
    size = lax.axis_size(axis)
    position = lax.axis_index(axis)
    chunk = block[:, 0]
    depth = 0
    for radix, stride in reversed(radix_stages(size)):
        digit = (position // stride) % radix
        received = [chunk]
        for shift in range(1, radix):
            route = []
            for source in range(size):
                own = (source // stride) % radix
                route.append((source, source + (((own + shift) % radix) - own) * stride))
            received.append(lax.ppermute(chunk, axis, route))
        stacked = jnp.stack(received)
        ordered = [stacked[(digit - origin) % radix] for origin in range(radix)]
        chunk = jnp.stack(ordered, axis=1 + depth)
        if depth == 0:
            first_stage = chunk
        depth += 1
    return chunk, first_stage


def group_reduce(value, axis, combine):
    size = lax.axis_size(axis)
    position = lax.axis_index(axis)
    total = value
    for radix, stride in radix_stages(size):
        digit = (position // stride) % radix
        received = [total]
        for shift in range(1, radix):
            route = []
            for source in range(size):
                own = (source // stride) % radix
                route.append((source, source + (((own + shift) % radix) - own) * stride))
            received.append(lax.ppermute(total, axis, route))
        stacked = jnp.stack(received)
        ordered = [stacked[(digit - origin) % radix] for origin in range(radix)]
        total = ordered[0]
        for part in ordered[1:]:
            total = combine(total, part)
    return total


def butterfly_reduce(value, axis, combine):
    size = lax.axis_size(axis)
    total = value
    stride = 1
    while stride < size:
        route = [(source, source ^ stride) for source in range(size)]
        total = combine(total, lax.ppermute(total, axis, route))
        stride *= 2
    return total


def from_behind(block, axis, distance):
    devices = range(lax.axis_size(axis))
    route = [(i - distance, i) for i in devices if i - distance in devices]
    return lax.ppermute(block, axis, route)


def block_mask(left_sizes, right_sizes, left_marks, right_marks, block_size):
    total = left_marks[:, None] + right_marks[None, :]
    allowed = (total == 4).astype(jnp.float32)
    offsets = jnp.arange(block_size, dtype=jnp.int32)
    live_rows = (offsets[None, :] < left_sizes[:, None]).astype(jnp.float32)
    live_cols = (offsets[None, :] < right_sizes[:, None]).astype(jnp.float32)
    return allowed[:, None, :, None] * live_rows[:, :, None, None] * live_cols[None, None, :, :]


def left_product(gathered):
    digits = gathered.shape[1:-2]
    letters = "dghijklm"[: len(digits)]
    spec = "w" + letters + "ac," + letters + "crb->w" + letters + "arb"

    def product(rounded):
        split = rounded.reshape(digits + rounded.shape[1:])
        done = jnp.einsum(spec, gathered, split, preferred_element_type=jnp.float32)
        return done.reshape((done.shape[0], rounded.shape[0]) + done.shape[-3:]).astype(jnp.bfloat16)

    return product


def hamiltonian(product, right_block, pattern):

    def apply_all(vector):
        left_done = product(vector.astype(jnp.bfloat16))
        return (
            jnp.einsum(
                "wqarc,wrbc->qarb", left_done, right_block, preferred_element_type=jnp.float32
            )
            * pattern
        )

    return apply_all


def operator_bound(left_peak, right_peak, block_size):
    bound = jnp.sum((block_size * left_peak) * (block_size * right_peak))
    bound = jnp.minimum(bound, jnp.finfo(jnp.float32).max)
    return jnp.where(bound > 0, bound, 1.0)


def krylov(first, apply_all, bound):
    basis = [first, apply_all(first)]
    for step in range(ITERS):
        basis.append(apply_all(basis[-1]) / bound)
    count = len(basis)
    pairs = [(i, j) for i in range(count) for j in range(i, count)]
    partial = jnp.stack([jnp.sum(basis[i] * basis[j]) for i, j in pairs])
    gram_sums = group_reduce(partial, "blk", lambda a, b: a + b)
    gram = [[None] * count for _ in range(count)]
    for index, (i, j) in enumerate(pairs):
        gram[i][j] = gram_sums[index]
        gram[j][i] = gram_sums[index]
    return basis, gram


def inner(gram, x, y):
    total = None
    for i, left in enumerate(x):
        if left is None:
            continue
        for j, right in enumerate(y):
            if right is None:
                continue
            term = left * gram[i][j] * right
            total = term if total is None else total + term
    return total


def combine(a, x, b, y):
    out = []
    for left, right in zip(x, y):
        if left is None and right is None:
            out.append(None)
        elif right is None:
            out.append(a * left)
        elif left is None:
            out.append(b * right)
        else:
            out.append(a * left + b * right)
    return out


def rotations(gram, bound):
    count = len(gram)
    one = jnp.ones((), jnp.float32)
    vector = [one] + [None] * (count - 1)
    image = [None, one] + [None] * (count - 2)
    ritz_value = inner(gram, vector, image)
    for sweep in range(ITERS):
        residual = combine(one, image, -ritz_value, vector)
        response = [None, residual[0]] + [
            None if part is None else bound * part for part in residual[1:-1]
        ]
        squared = inner(gram, residual, residual) + EPS
        coupling = inner(gram, residual, response) / squared
        midpoint = 0.5 * (ritz_value - coupling)
        radius = jnp.sqrt(midpoint * midpoint + squared)
        cosine = jnp.sqrt(0.5 * (1.0 - midpoint / radius))
        sine_value = -jnp.sqrt(0.5 * (1.0 + midpoint / radius))
        length = jnp.sqrt(squared)
        vector = combine(cosine, vector, sine_value / length, residual)
        image = combine(cosine, image, sine_value / length, response)
        ritz_value = 0.5 * (ritz_value + coupling) - radius
    return vector, ritz_value


def davidson(first, apply_all, bound):
    basis, gram = krylov(first, apply_all, bound)
    weights, ritz_value = rotations(gram, bound)
    vector = None
    for weight, part in zip(weights, basis):
        if weight is None:
            continue
        vector = weight * part if vector is None else vector + weight * part
    norm_sq = inner(gram, weights, weights)
    return vector, ritz_value, norm_sq


def refresh(vector, product, states):
    rounded = vector.astype(jnp.bfloat16)
    left_done = product(rounded)
    return (
        states
        * jnp.einsum("qarb,wqarc->wrbc", rounded, left_done, preferred_element_type=jnp.float32)
    ).astype(jnp.bfloat16)


def peak(block):
    return jnp.max(jnp.abs(block.astype(jnp.float32)), axis=tuple(range(1, block.ndim)))


def local(guess, left_env, right_env, left_dims, right_dims, left_labels, right_labels):
    start_guess = guess[0].astype(jnp.float32)
    left_block = left_env[0]
    right_block = right_env[0]
    sector_count = start_guess.shape[0]
    block_size = start_guess.shape[1]
    owned_count = start_guess.shape[2]
    states = sector_count * block_size
    first_owned = lax.axis_index("blk") * owned_count
    owned_sizes = lax.dynamic_slice_in_dim(right_dims[0], first_owned, owned_count, 0)
    owned_marks = lax.dynamic_slice_in_dim(right_labels[0], first_owned, owned_count, 0)
    pattern = block_mask(left_dims[0], owned_sizes, left_labels[0], owned_marks, block_size)
    masked = start_guess * pattern
    first_gathered, first_stage = group_gather(left_block, "blk")
    after_stage = first_stage[0, 0, 0, 0].astype(jnp.float32) * 0.0
    early = butterfly_reduce(
        jnp.concatenate([jnp.sum(masked * masked)[None], peak(right_block)]) + after_stage,
        "blk",
        lambda a, b: jnp.concatenate([a[:1] + b[:1], jnp.maximum(a[1:], b[1:])]),
    )
    right_peak = early[1:]
    first_product = left_product(first_gathered)
    first_bound = operator_bound(peak(first_gathered), right_peak, block_size)
    first_start = masked / jnp.sqrt(early[0] + EPS)
    first_vector, first_energy, first_norm = davidson(
        first_start, hamiltonian(first_product, right_block, pattern), first_bound
    )
    fresh = refresh(first_vector, first_product, states)
    passed = from_behind(fresh, "sec", 1)
    second_left = jnp.where(lax.axis_index("sec") == 0, left_block, passed)
    second_gathered, _ = group_gather(second_left, "blk")
    second_product = left_product(second_gathered)
    second_bound = operator_bound(peak(second_gathered), right_peak, block_size)
    second_start = first_vector * pattern / jnp.sqrt(first_norm + EPS)
    second_vector, second_energy, _ = davidson(
        second_start, hamiltonian(second_product, right_block, pattern), second_bound
    )
    waves = (states * second_vector)[None]
    energies = jnp.stack([first_energy, second_energy])[None]
    return (waves, energies)


def solution(mesh):
    return jax.shard_map(
        local,
        mesh=mesh,
        in_specs=(
            P("sec", None, None, "blk", None),
            P("sec", None, "blk", None, None),
            P("sec", None, "blk", None, None),
            P("sec", None),
            P("sec", None),
            P("sec", None),
            P("sec", None),
        ),
        out_specs=(P("sec", None, None, "blk", None), P("sec", None)),
        check_vma=False,
    )
```

```python
import jax
import jax.numpy as jnp
from jax import lax
from jax.sharding import PartitionSpec as P

ITERS = 2


EPS = 1e-06


def radix_stages(size):
    stages = []
    stride = 1
    for radix in (2, 4, 4, 2, 2, 2, 2):
        if stride >= size:
            break
        if size % (stride * radix):
            radix = 2
        stages.append((radix, stride))
        stride *= radix
    return stages


def group_gather(block, axis):
    size = lax.axis_size(axis)
    position = lax.axis_index(axis)
    chunk = block[:, 0]
    depth = 0
    for radix, stride in reversed(radix_stages(size)):
        digit = (position // stride) % radix
        received = [chunk]
        for shift in range(1, radix):
            route = []
            for source in range(size):
                own = (source // stride) % radix
                route.append((source, source + (((own + shift) % radix) - own) * stride))
            received.append(lax.ppermute(chunk, axis, route))
        stacked = jnp.stack(received)
        ordered = [stacked[(digit - origin) % radix] for origin in range(radix)]
        chunk = jnp.stack(ordered, axis=1 + depth)
        if depth == 0:
            first_stage = chunk
        depth += 1
    return chunk, first_stage


def group_reduce(value, axis, combine, widest_first=False):
    size = lax.axis_size(axis)
    position = lax.axis_index(axis)
    total = value
    stages = radix_stages(size)
    for radix, stride in (stages[::-1] if widest_first else stages):
        digit = (position // stride) % radix
        received = [total]
        for shift in range(1, radix):
            route = []
            for source in range(size):
                own = (source // stride) % radix
                route.append((source, source + (((own + shift) % radix) - own) * stride))
            received.append(lax.ppermute(total, axis, route))
        stacked = jnp.stack(received)
        ordered = [stacked[(digit - origin) % radix] for origin in range(radix)]
        total = ordered[0]
        for part in ordered[1:]:
            total = combine(total, part)
    return total


def from_behind(block, axis, distance):
    devices = range(lax.axis_size(axis))
    route = [(i - distance, i) for i in devices if i - distance in devices]
    return lax.ppermute(block, axis, route)


def block_mask(left_sizes, right_sizes, left_marks, right_marks, block_size):
    total = left_marks[:, None] + right_marks[None, :]
    allowed = (total == 4).astype(jnp.float32)
    offsets = jnp.arange(block_size, dtype=jnp.int32)
    live_rows = (offsets[None, :] < left_sizes[:, None]).astype(jnp.float32)
    live_cols = (offsets[None, :] < right_sizes[:, None]).astype(jnp.float32)
    return allowed[:, None, :, None] * live_rows[:, :, None, None] * live_cols[None, None, :, :]


def left_product(gathered):
    digits = gathered.shape[1:-2]
    letters = "dghijklm"[: len(digits)]
    spec = "w" + letters + "ac," + letters + "crb->w" + letters + "arb"

    def product(rounded):
        split = rounded.reshape(digits + rounded.shape[1:])
        done = jnp.einsum(spec, gathered, split, preferred_element_type=jnp.float32)
        return done.reshape((done.shape[0], rounded.shape[0]) + done.shape[-3:]).astype(jnp.bfloat16)

    return product


def hamiltonian(product, right_block, pattern):

    def apply_all(vector):
        left_done = product(vector.astype(jnp.bfloat16))
        return (
            jnp.einsum(
                "wqarc,wrbc->qarb", left_done, right_block, preferred_element_type=jnp.float32
            )
            * pattern
        )

    return apply_all


def operator_bound(left_peak, right_peak, block_size):
    bound = jnp.sum((block_size * left_peak) * (block_size * right_peak))
    bound = jnp.minimum(bound, jnp.finfo(jnp.float32).max)
    return jnp.where(bound > 0, bound, 1.0)


def krylov(first, apply_all, bound):
    basis = [first, apply_all(first)]
    for step in range(ITERS):
        basis.append(apply_all(basis[-1]) / bound)
    count = len(basis)
    pairs = [(i, j) for i in range(count) for j in range(i, count)]
    partial = jnp.stack([jnp.sum(basis[i] * basis[j]) for i, j in pairs])
    gram_sums = group_reduce(partial, "blk", lambda a, b: a + b, widest_first=True)
    gram = [[None] * count for _ in range(count)]
    for index, (i, j) in enumerate(pairs):
        gram[i][j] = gram_sums[index]
        gram[j][i] = gram_sums[index]
    return basis, gram


def inner(gram, x, y):
    total = None
    for i, left in enumerate(x):
        if left is None:
            continue
        for j, right in enumerate(y):
            if right is None:
                continue
            term = left * gram[i][j] * right
            total = term if total is None else total + term
    return total


def combine(a, x, b, y):
    out = []
    for left, right in zip(x, y):
        if left is None and right is None:
            out.append(None)
        elif right is None:
            out.append(a * left)
        elif left is None:
            out.append(b * right)
        else:
            out.append(a * left + b * right)
    return out


def rotations(gram, bound):
    count = len(gram)
    one = jnp.ones((), jnp.float32)
    vector = [one] + [None] * (count - 1)
    image = [None, one] + [None] * (count - 2)
    ritz_value = inner(gram, vector, image)
    for sweep in range(ITERS):
        residual = combine(one, image, -ritz_value, vector)
        response = [None, residual[0]] + [
            None if part is None else bound * part for part in residual[1:-1]
        ]
        squared = inner(gram, residual, residual) + EPS
        coupling = inner(gram, residual, response) / squared
        midpoint = 0.5 * (ritz_value - coupling)
        radius = jnp.sqrt(midpoint * midpoint + squared)
        cosine = jnp.sqrt(0.5 * (1.0 - midpoint / radius))
        sine_value = -jnp.sqrt(0.5 * (1.0 + midpoint / radius))
        length = jnp.sqrt(squared)
        vector = combine(cosine, vector, sine_value / length, residual)
        image = combine(cosine, image, sine_value / length, response)
        ritz_value = 0.5 * (ritz_value + coupling) - radius
    return vector, ritz_value


def davidson(first, apply_all, bound):
    basis, gram = krylov(first, apply_all, bound)
    weights, ritz_value = rotations(gram, bound)
    vector = None
    for weight, part in zip(weights, basis):
        if weight is None:
            continue
        vector = weight * part if vector is None else vector + weight * part
    norm_sq = inner(gram, weights, weights)
    return vector, ritz_value, norm_sq


def refresh(vector, product, states):
    rounded = vector.astype(jnp.bfloat16)
    left_done = product(rounded)
    return (
        states
        * jnp.einsum("qarb,wqarc->wrbc", rounded, left_done, preferred_element_type=jnp.float32)
    ).astype(jnp.bfloat16)


def peak(block):
    return jnp.max(jnp.abs(block.astype(jnp.float32)), axis=tuple(range(1, block.ndim)))


def local(guess, left_env, right_env, left_dims, right_dims, left_labels, right_labels):
    start_guess = guess[0].astype(jnp.float32)
    left_block = left_env[0]
    right_block = right_env[0]
    sector_count = start_guess.shape[0]
    block_size = start_guess.shape[1]
    owned_count = start_guess.shape[2]
    states = sector_count * block_size
    first_owned = lax.axis_index("blk") * owned_count
    owned_sizes = lax.dynamic_slice_in_dim(right_dims[0], first_owned, owned_count, 0)
    owned_marks = lax.dynamic_slice_in_dim(right_labels[0], first_owned, owned_count, 0)
    pattern = block_mask(left_dims[0], owned_sizes, left_labels[0], owned_marks, block_size)
    masked = start_guess * pattern
    first_gathered, first_stage = group_gather(left_block, "blk")
    after_stage = first_stage[0, 0, 0, 0].astype(jnp.float32) * 0.0
    early = group_reduce(
        jnp.concatenate([jnp.sum(masked * masked)[None], peak(right_block)]) + after_stage,
        "blk",
        lambda a, b: jnp.concatenate([a[:1] + b[:1], jnp.maximum(a[1:], b[1:])]),
    )
    right_peak = early[1:]
    first_product = left_product(first_gathered)
    first_bound = operator_bound(peak(first_gathered), right_peak, block_size)
    first_start = masked / jnp.sqrt(early[0] + EPS)
    first_vector, first_energy, first_norm = davidson(
        first_start, hamiltonian(first_product, right_block, pattern), first_bound
    )
    fresh = refresh(first_vector, first_product, states)
    passed = from_behind(fresh, "sec", 1)
    second_left = jnp.where(lax.axis_index("sec") == 0, left_block, passed)
    second_gathered, _ = group_gather(second_left, "blk")
    second_product = left_product(second_gathered)
    second_bound = operator_bound(peak(second_gathered), right_peak, block_size)
    second_start = first_vector * pattern / jnp.sqrt(first_norm + EPS)
    second_vector, second_energy, _ = davidson(
        second_start, hamiltonian(second_product, right_block, pattern), second_bound
    )
    waves = (states * second_vector)[None]
    energies = jnp.stack([first_energy, second_energy])[None]
    return (waves, energies)


def solution(mesh):
    return jax.shard_map(
        local,
        mesh=mesh,
        in_specs=(
            P("sec", None, None, "blk", None),
            P("sec", None, "blk", None, None),
            P("sec", None, "blk", None, None),
            P("sec", None),
            P("sec", None),
            P("sec", None),
            P("sec", None),
        ),
        out_specs=(P("sec", None, None, "blk", None), P("sec", None)),
        check_vma=False,
    )
```
